256 devices in a mesh: node: 8 (over z_lo, core), drow: 4 (over x), dcol: 8 (over z_hi, y).
Axes of the slice: x: 4, y: 4, z: 8 (z_hi: 2, z_lo: 4; z = z_hi * 4 + z_lo), core: 2. Of those that a mesh axis runs over, the one named last changes fastest.
Arguments:
- freq_resp: bfloat16 [2, 8, 4096, 8192], P(None, None, ('drow', 'dcol'), 'node'), may hold values from -0.0625 to 0.0625
- node_coords: int32 [2, 8192], P(None, 'node'), may hold values from 0 to 1023
- heading_steps: int32 [2, 512], replicated, may hold values from -8 to 8
- spectral_weights: int32 [8, 512], replicated, may hold values from 1 to 64
Outputs:
- cross_spectra: float32 [2, 8, 4, 1024, 4096], P(None, None, 'drow', 'node', 'dcol')
The draws below stay inside these ranges and needn't reach their ends.
All inputs are finite; a program needn't handle non-finite values.
Results may differ from the reference program's by a relative error of at most 0.0038.
Values may be sent and summed in bfloat16 or wider, within the bound.
No kernel may reach another device: no remote copies, remote signals or barrier semaphores. Data moves between devices by JAX's collectives and lax.ppermute only.
A program may use at most 128 MiB of HBM per device.

```python
import math
import jax
import jax.numpy as jnp

DOF = 4096
DIRS = 512
FREQS = 8
GRID = 1024
NODES = 8192
N_NODE = 8
N_DROW = 4
N_DCOL = 8


def set_ends(array, stream_key, least, top_value):
    extent = array.shape
    spot = [jax.random.randint(jax.random.fold_in(stream_key, axis), (), 0, extent[axis]) for axis in range(len(extent))]
    array = array.at[tuple(spot)].set(least)
    longest = extent.index(max(extent))
    spot[longest] = (spot[longest] + 1) % extent[longest]
    return array.at[tuple(spot)].set(top_value)


def level_of(stream_key, shape, shards, least, largest):
    gain = 1.0
    for dim, parts in shards:
        steps = jax.random.uniform(jax.random.fold_in(jax.random.fold_in(stream_key, 6), dim), (parts,), jnp.float32, least / len(shards), largest / len(shards))
        gain = gain * jnp.repeat(jnp.exp(steps), shape[dim] // parts).reshape((-1,) + (1,) * (len(shape) - 1 - dim))
    return gain


def scatter_about(rng, extent, scale, reach, cuts=(), held_as=jnp.bfloat16):
    loudness = level_of(rng, extent, cuts, -0.22, 0.18) if cuts else 1.0
    array = jax.random.normal(rng, extent, jnp.float32) * scale * loudness
    return jnp.minimum(jnp.maximum(array, -reach), reach).astype(held_as)


def setup_inputs(seed: int = 0) -> dict:
    arg_keys = jax.random.split(jax.random.key(seed), 5)
    freq_resp = scatter_about(arg_keys[0], (2, FREQS, DOF, NODES), NODES ** -0.5, 0.0625, ((2, 32), (3, 8)))
    node_coords = set_ends(jax.random.randint(arg_keys[1], (2, NODES), 0, GRID), jax.random.fold_in(arg_keys[1], 1), 0, GRID - 1).astype(jnp.int32)
    heading_steps = set_ends(jax.random.randint(arg_keys[2], (2, DIRS), -8, 9), jax.random.fold_in(arg_keys[2], 1), -8, 8).astype(jnp.int32)
    spectral_weights = set_ends(jax.random.randint(arg_keys[3], (FREQS, DIRS), 1, 65), jax.random.fold_in(arg_keys[3], 1), 1, 64).astype(jnp.int32)
    return {"freq_resp": freq_resp, "node_coords": node_coords, "heading_steps": heading_steps, "spectral_weights": spectral_weights}


def excitation(coords, heading_steps, spectral_weights):
    freq_index = (jnp.arange(FREQS, dtype=jnp.int32) + 1)[:, None, None]
    project = coords[0][:, None] * heading_steps[0][None, :] + coords[1][:, None] * heading_steps[1][None, :]
    turn_count = jnp.mod(freq_index * project[None], GRID)
    phase_angle = turn_count.astype(jnp.float32) * (2.0 * math.pi / GRID)
    spread = jnp.sqrt(spectral_weights.astype(jnp.float32) / (64.0 * DIRS))[:, None, :]
    load_re = (spread * jnp.cos(phase_angle)).astype(jnp.bfloat16)
    load_im = (-spread * jnp.sin(phase_angle)).astype(jnp.bfloat16)
    return (load_re, load_im)

def row_order(matrix):
    slice_rows = DOF // (N_DROW * N_DCOL * N_NODE)
    shaped = matrix.reshape(N_DROW, N_DCOL, N_NODE, slice_rows, DIRS)
    return shaped.transpose(0, 2, 1, 3, 4).reshape(DOF, DIRS)

def col_order(matrix):
    slice_rows = DOF // (N_DROW * N_DCOL * N_NODE)
    shaped = matrix.reshape(N_DROW, N_DCOL, N_NODE, slice_rows, DIRS)
    return shaped.transpose(1, 2, 0, 3, 4).reshape(DOF, DIRS)

def reference(freq_resp, node_coords, heading_steps, spectral_weights):
    load_re, load_im = excitation(node_coords, heading_steps, spectral_weights)
    results = []
    for freq_index in range(FREQS):
        resp_re = freq_resp[0, freq_index]
        resp_im = freq_resp[1, freq_index]
        amp_re = (jnp.dot(resp_re, load_re[freq_index], preferred_element_type=jnp.float32) - jnp.dot(resp_im, load_im[freq_index], preferred_element_type=jnp.float32)).astype(jnp.bfloat16)
        amp_im = (jnp.dot(resp_re, load_im[freq_index], preferred_element_type=jnp.float32) + jnp.dot(resp_im, load_re[freq_index], preferred_element_type=jnp.float32)).astype(jnp.bfloat16)
        row_re = row_order(amp_re)
        row_im = row_order(amp_im)
        col_re = col_order(amp_re)
        col_im = col_order(amp_im)
        spec_re = jnp.dot(row_re, col_re.T, preferred_element_type=jnp.float32) + jnp.dot(row_im, col_im.T, preferred_element_type=jnp.float32)
        spec_im = jnp.dot(row_im, col_re.T, preferred_element_type=jnp.float32) - jnp.dot(row_re, col_im.T, preferred_element_type=jnp.float32)
        results.append(jnp.stack([spec_re, spec_im]))
    stacked = jnp.stack(results, axis=1)
    return stacked.reshape(2, FREQS, N_DROW, DOF // N_DROW, DOF)
```

```python
import math

import jax
import jax.numpy as jnp
from jax import lax
from jax.sharding import PartitionSpec as P

DIRS = 512
FREQS = 8
GRID = 1024


def unit_phasor(turn):
    quarter = GRID // 4
    shifted = (turn + quarter // 2) & (GRID - 1)
    quadrant = shifted >> 8
    offset = (shifted & (quarter - 1)) - quarter // 2
    x = offset.astype(jnp.float32) * (2.0 * math.pi / GRID)
    x2 = x * x
    s = x * (1.0 + x2 * (-1.0 / 6 + x2 * (1.0 / 120 + x2 * (-1.0 / 5040 + x2 * (1.0 / 362880)))))
    c = 1.0 + x2 * (-0.5 + x2 * (1.0 / 24 + x2 * (-1.0 / 720 + x2 * (1.0 / 40320))))
    odd = (quadrant & 1) == 1
    cos_mag = jnp.where(odd, s, c)
    sin_mag = jnp.where(odd, c, s)
    cos_neg = (quadrant == 1) | (quadrant == 2)
    sin_neg = quadrant >= 2
    return jnp.where(cos_neg, -cos_mag, cos_mag), jnp.where(sin_neg, -sin_mag, sin_mag)


def excitation(coords, heading_steps, spectral_weights):
    freq_index = (jnp.arange(FREQS, dtype=jnp.int32) + 1)[:, None, None]
    project = (
        coords[0][:, None] * heading_steps[0][None, :]
        + coords[1][:, None] * heading_steps[1][None, :]
    )
    turn_count = (freq_index * project[None]) & (GRID - 1)
    cos_t, sin_t = unit_phasor(turn_count)
    spread = jnp.sqrt(spectral_weights.astype(jnp.float32) / (64.0 * DIRS))[:, None, :]
    load_re = (spread * cos_t).astype(jnp.bfloat16)
    load_im = (-spread * sin_t).astype(jnp.bfloat16)
    return load_re, load_im


def local(freq_resp, node_coords, heading_steps, spectral_weights):
    load_re, load_im = excitation(node_coords, heading_steps, spectral_weights)
    right = jnp.stack(
        [
            jnp.concatenate([load_re, load_im], axis=-1),
            jnp.concatenate([-load_im, load_re], axis=-1),
        ],
        axis=0,
    )
    partial_amp = jnp.einsum(
        "pfkn,pfne->fke", freq_resp, right, preferred_element_type=jnp.float32
    )
    amplitudes = lax.psum_scatter(partial_amp, "node", scatter_dimension=1, tiled=True).astype(
        jnp.bfloat16
    )
    cols = lax.all_gather(amplitudes, ("node", "drow"), axis=1, tiled=True)
    rows = lax.all_gather(amplitudes, "dcol", axis=1, tiled=True)
    rows_im = jnp.concatenate([rows[..., DIRS:], -rows[..., :DIRS]], axis=-1)
    lead = jnp.stack([rows, rows_im], axis=0)
    spec = jnp.einsum("pfke,fje->pfkj", lead, cols, preferred_element_type=jnp.float32)
    return spec[:, :, None]


def solution(mesh):
    placed = (P(None, None, ("drow", "dcol"), "node"), P(None, "node"), P(), P())
    return jax.shard_map(
        local,
        mesh=mesh,
        in_specs=placed,
        out_specs=P(None, None, "drow", "node", "dcol"),
        check_vma=False,
    )
```

```python
import math

import jax
import jax.numpy as jnp
from jax import lax
from jax.experimental import pallas as pl
from jax.experimental.pallas import tpu as pltpu
from jax.sharding import PartitionSpec as P

DIRS = 512
FREQS = 8
GRID = 1024
NODE_TILE = 256


def unit_phasor(turn):
    quarter = GRID // 4
    shifted = (turn + quarter // 2) & (GRID - 1)
    quadrant = shifted >> 8
    offset = (shifted & (quarter - 1)) - quarter // 2
    x = offset.astype(jnp.float32) * (2.0 * math.pi / GRID)
    x2 = x * x
    s = x * (1.0 + x2 * (-1.0 / 6 + x2 * (1.0 / 120 + x2 * (-1.0 / 5040 + x2 * (1.0 / 362880)))))
    c = 1.0 + x2 * (-0.5 + x2 * (1.0 / 24 + x2 * (-1.0 / 720 + x2 * (1.0 / 40320))))
    odd = (quadrant & 1) == 1
    cos_mag = jnp.where(odd, s, c)
    sin_mag = jnp.where(odd, c, s)
    cos_neg = (quadrant == 1) | (quadrant == 2)
    sin_neg = quadrant >= 2
    return jnp.where(cos_neg, -cos_mag, cos_mag), jnp.where(sin_neg, -sin_mag, sin_mag)


def amp_kernel(proj_ref, spread_ref, resp_ref, out_ref):
    @pl.when(pl.program_id(0) == 0)
    def _():
        out_ref[...] = jnp.zeros_like(out_ref)

    proj = proj_ref[...]
    base_c, base_s = unit_phasor(proj & (GRID - 1))
    rows = resp_ref.shape[2]
    cos_f, sin_f = base_c, base_s
    for f in range(FREQS):
        if f > 0:
            cos_f, sin_f = (
                cos_f * base_c - sin_f * base_s,
                sin_f * base_c + cos_f * base_s,
            )
        spread = spread_ref[f : f + 1, :]
        load_re = (spread * cos_f).astype(jnp.bfloat16)
        load_im = (-spread * sin_f).astype(jnp.bfloat16)
        resp = resp_ref[:, f].reshape(2 * rows, resp_ref.shape[3])
        by_re = jnp.dot(resp, load_re, preferred_element_type=jnp.float32)
        by_im = jnp.dot(resp, load_im, preferred_element_type=jnp.float32)
        out_ref[f, :, :DIRS] += by_re[:rows] - by_im[rows:]
        out_ref[f, :, DIRS:] += by_im[:rows] + by_re[rows:]


def partial_amplitudes(freq_resp, project, spread):
    nodes = project.shape[0]
    rows = freq_resp.shape[2]
    return pl.pallas_call(
        amp_kernel,
        out_shape=jax.ShapeDtypeStruct((FREQS, rows, 2 * DIRS), jnp.float32),
        grid=(nodes // NODE_TILE,),
        in_specs=[
            pl.BlockSpec((NODE_TILE, DIRS), lambda j: (j, 0)),
            pl.BlockSpec((FREQS, DIRS), lambda j: (0, 0)),
            pl.BlockSpec((2, FREQS, rows, NODE_TILE), lambda j: (0, 0, 0, j)),
        ],
        out_specs=pl.BlockSpec((FREQS, rows, 2 * DIRS), lambda j: (0, 0, 0)),
        compiler_params=pltpu.CompilerParams(dimension_semantics=("arbitrary",)),
    )(project, spread, freq_resp)


def local(freq_resp, node_coords, heading_steps, spectral_weights):
    project = (
        node_coords[0][:, None] * heading_steps[0][None, :]
        + node_coords[1][:, None] * heading_steps[1][None, :]
    )
    spread = jnp.sqrt(spectral_weights.astype(jnp.float32) / (64.0 * DIRS))
    partial_amp = partial_amplitudes(freq_resp, project, spread)
    amplitudes = lax.psum_scatter(partial_amp, "node", scatter_dimension=1, tiled=True).astype(
        jnp.bfloat16
    )
    cols = lax.all_gather(amplitudes, ("node", "drow"), axis=1, tiled=True)
    rows = lax.all_gather(amplitudes, "dcol", axis=1, tiled=True)
    rows_im = jnp.concatenate([rows[..., DIRS:], -rows[..., :DIRS]], axis=-1)
    lead = jnp.stack([rows, rows_im], axis=0)
    spec = jnp.einsum("pfke,fje->pfkj", lead, cols, preferred_element_type=jnp.float32)
    return spec[:, :, None]


def solution(mesh):
    placed = (P(None, None, ("drow", "dcol"), "node"), P(None, "node"), P(), P())
    return jax.shard_map(
        local,
        mesh=mesh,
        in_specs=placed,
        out_specs=P(None, None, "drow", "node", "dcol"),
        check_vma=False,
    )
```

```python
import math

import jax
import jax.numpy as jnp
from jax import lax
from jax.experimental import pallas as pl
from jax.experimental.pallas import tpu as pltpu
from jax.sharding import PartitionSpec as P

DIRS = 512
FREQS = 8
GRID = 1024
NODE_TILE = 256


def unit_phasor(turn):
    quarter = GRID // 4
    shifted = (turn + quarter // 2) & (GRID - 1)
    quadrant = shifted >> 8
    offset = (shifted & (quarter - 1)) - quarter // 2
    x = offset.astype(jnp.float32) * (2.0 * math.pi / GRID)
    x2 = x * x
    s = x * (1.0 + x2 * (-1.0 / 6 + x2 * (1.0 / 120 + x2 * (-1.0 / 5040 + x2 * (1.0 / 362880)))))
    c = 1.0 + x2 * (-0.5 + x2 * (1.0 / 24 + x2 * (-1.0 / 720 + x2 * (1.0 / 40320))))
    odd = (quadrant & 1) == 1
    cos_mag = jnp.where(odd, s, c)
    sin_mag = jnp.where(odd, c, s)
    cos_neg = (quadrant == 1) | (quadrant == 2)
    sin_neg = quadrant >= 2
    return jnp.where(cos_neg, -cos_mag, cos_mag), jnp.where(sin_neg, -sin_mag, sin_mag)


def amp_kernel(proj_ref, spread_ref, resp_ref, out_ref):
    @pl.when(pl.program_id(0) == 0)
    def _():
        out_ref[...] = jnp.zeros_like(out_ref)

    proj = proj_ref[...]
    base_c, base_s = unit_phasor(proj & (GRID - 1))
    rows = resp_ref.shape[2]
    cos_f, sin_f = base_c, base_s
    for f in range(FREQS):
        if f > 0:
            cos_f, sin_f = (
                cos_f * base_c - sin_f * base_s,
                sin_f * base_c + cos_f * base_s,
            )
        spread = spread_ref[f : f + 1, :]
        load_re = (spread * cos_f).astype(jnp.bfloat16)
        load_im = (-spread * sin_f).astype(jnp.bfloat16)
        resp = resp_ref[:, f].reshape(2 * rows, resp_ref.shape[3])
        by_re = jnp.dot(resp, load_re, preferred_element_type=jnp.float32)
        by_im = jnp.dot(resp, load_im, preferred_element_type=jnp.float32)
        out_ref[f, :, :DIRS] += by_re[:rows] - by_im[rows:]
        out_ref[f, :, DIRS:] += by_im[:rows] + by_re[rows:]


def partial_amplitudes(freq_resp, project, spread):
    nodes = project.shape[0]
    rows = freq_resp.shape[2]
    return pl.pallas_call(
        amp_kernel,
        out_shape=jax.ShapeDtypeStruct((FREQS, rows, 2 * DIRS), jnp.float32),
        grid=(nodes // NODE_TILE,),
        in_specs=[
            pl.BlockSpec((NODE_TILE, DIRS), lambda j: (j, 0)),
            pl.BlockSpec((FREQS, DIRS), lambda j: (0, 0)),
            pl.BlockSpec((2, FREQS, rows, NODE_TILE), lambda j: (0, 0, 0, j)),
        ],
        out_specs=pl.BlockSpec((FREQS, rows, 2 * DIRS), lambda j: (0, 0, 0)),
        compiler_params=pltpu.CompilerParams(dimension_semantics=("arbitrary",)),
    )(project, spread, freq_resp)


def gather_rows(amplitudes):
    count = lax.axis_size("dcol")
    ahead = [amplitudes]
    for shift in range(1, count):
        ahead.append(
            lax.ppermute(
                amplitudes, "dcol", perm=[(i, (i - shift) % count) for i in range(count)]
            )
        )
    stacked = jnp.stack(ahead, axis=1)
    rolled = jnp.roll(stacked, lax.axis_index("dcol"), axis=1)
    return rolled.reshape(stacked.shape[0], -1, stacked.shape[-1])


def local(freq_resp, node_coords, heading_steps, spectral_weights):
    project = (
        node_coords[0][:, None] * heading_steps[0][None, :]
        + node_coords[1][:, None] * heading_steps[1][None, :]
    )
    spread = jnp.sqrt(spectral_weights.astype(jnp.float32) / (64.0 * DIRS))
    partial_amp = partial_amplitudes(freq_resp, project, spread)
    amplitudes = lax.psum_scatter(partial_amp, "node", scatter_dimension=1, tiled=True).astype(
        jnp.bfloat16
    )
    cols = lax.all_gather(amplitudes, ("node", "drow"), axis=1, tiled=True)
    rows = gather_rows(amplitudes)
    rows_im = jnp.concatenate([rows[..., DIRS:], -rows[..., :DIRS]], axis=-1)
    lead = jnp.stack([rows, rows_im], axis=0)
    spec = jnp.einsum("pfke,fje->pfkj", lead, cols, preferred_element_type=jnp.float32)
    return spec[:, :, None]


def solution(mesh):
    placed = (P(None, None, ("drow", "dcol"), "node"), P(None, "node"), P(), P())
    return jax.shard_map(
        local,
        mesh=mesh,
        in_specs=placed,
        out_specs=P(None, None, "drow", "node", "dcol"),
        check_vma=False,
    )
```

```python
import math

import jax
import jax.numpy as jnp
from jax import lax
from jax.experimental import pallas as pl
from jax.experimental.pallas import tpu as pltpu
from jax.sharding import PartitionSpec as P

DIRS = 512
FREQS = 8
GRID = 1024
NODE_TILE = 256


def unit_phasor(turn):
    quarter = GRID // 4
    shifted = (turn + quarter // 2) & (GRID - 1)
    quadrant = shifted >> 8
    offset = (shifted & (quarter - 1)) - quarter // 2
    x = offset.astype(jnp.float32) * (2.0 * math.pi / GRID)
    x2 = x * x
    s = x * (1.0 + x2 * (-1.0 / 6 + x2 * (1.0 / 120 + x2 * (-1.0 / 5040 + x2 * (1.0 / 362880)))))
    c = 1.0 + x2 * (-0.5 + x2 * (1.0 / 24 + x2 * (-1.0 / 720 + x2 * (1.0 / 40320))))
    odd = (quadrant & 1) == 1
    cos_mag = jnp.where(odd, s, c)
    sin_mag = jnp.where(odd, c, s)
    cos_neg = (quadrant == 1) | (quadrant == 2)
    sin_neg = quadrant >= 2
    return jnp.where(cos_neg, -cos_mag, cos_mag), jnp.where(sin_neg, -sin_mag, sin_mag)


def amp_kernel(proj_ref, spread_ref, resp_ref, out_ref):
    @pl.when(pl.program_id(0) == 0)
    def _():
        out_ref[...] = jnp.zeros_like(out_ref)

    proj = proj_ref[...]
    base_c, base_s = unit_phasor(proj & (GRID - 1))
    rows = resp_ref.shape[2]
    cos_f, sin_f = base_c, base_s
    for f in range(FREQS):
        if f > 0:
            cos_f, sin_f = (
                cos_f * base_c - sin_f * base_s,
                sin_f * base_c + cos_f * base_s,
            )
        spread = spread_ref[f : f + 1, :]
        load_re = (spread * cos_f).astype(jnp.bfloat16)
        load_im = (-spread * sin_f).astype(jnp.bfloat16)
        resp = resp_ref[:, f].reshape(2 * rows, resp_ref.shape[3])
        by_re = jnp.dot(resp, load_re, preferred_element_type=jnp.float32)
        by_im = jnp.dot(resp, load_im, preferred_element_type=jnp.float32)
        out_ref[f, :, :DIRS] += by_re[:rows] - by_im[rows:]
        out_ref[f, :, DIRS:] += by_im[:rows] + by_re[rows:]


def partial_amplitudes(freq_resp, project, spread):
    nodes = project.shape[0]
    rows = freq_resp.shape[2]
    return pl.pallas_call(
        amp_kernel,
        out_shape=jax.ShapeDtypeStruct((FREQS, rows, 2 * DIRS), jnp.float32),
        grid=(nodes // NODE_TILE,),
        in_specs=[
            pl.BlockSpec((NODE_TILE, DIRS), lambda j: (j, 0)),
            pl.BlockSpec((FREQS, DIRS), lambda j: (0, 0)),
            pl.BlockSpec((2, FREQS, rows, NODE_TILE), lambda j: (0, 0, 0, j)),
        ],
        out_specs=pl.BlockSpec((FREQS, rows, 2 * DIRS), lambda j: (0, 0, 0)),
        compiler_params=pltpu.CompilerParams(dimension_semantics=("arbitrary",)),
    )(project, spread, freq_resp)


def gather_cols(amplitudes):
    freqs, piece, width = amplitudes.shape
    along_z = lax.all_gather(amplitudes, "zlo", axis=1, tiled=True)
    along_z = along_z.reshape(freqs, -1, piece, width)
    mine = lax.all_gather(along_z, "drow", axis=2)
    theirs = lax.ppermute(mine, "core", perm=[(0, 1), (1, 0)])
    first = lax.axis_index("core") == 0
    pair = jnp.where(first, jnp.stack([mine, theirs], axis=2), jnp.stack([theirs, mine], axis=2))
    return pair.reshape(freqs, -1, width)


def gather_rows(amplitudes):
    count = lax.axis_size("zhi") * lax.axis_size("y")
    ahead = [amplitudes]
    for shift in range(1, count):
        ahead.append(
            lax.ppermute(
                amplitudes, ("zhi", "y"), perm=[(i, (i - shift) % count) for i in range(count)]
            )
        )
    stacked = jnp.stack(ahead, axis=1)
    rolled = jnp.roll(stacked, lax.axis_index(("zhi", "y")), axis=1)
    return rolled.reshape(stacked.shape[0], -1, stacked.shape[-1])


def local(freq_resp, node_coords, heading_steps, spectral_weights):
    project = (
        node_coords[0][:, None] * heading_steps[0][None, :]
        + node_coords[1][:, None] * heading_steps[1][None, :]
    )
    spread = jnp.sqrt(spectral_weights.astype(jnp.float32) / (64.0 * DIRS))
    partial_amp = partial_amplitudes(freq_resp, project, spread)
    amplitudes = lax.psum_scatter(partial_amp, ("zlo", "core"), scatter_dimension=1, tiled=True).astype(
        jnp.bfloat16
    )
    cols = gather_cols(amplitudes)
    rows = gather_rows(amplitudes)
    rows_im = jnp.concatenate([rows[..., DIRS:], -rows[..., :DIRS]], axis=-1)
    lead = jnp.stack([rows, rows_im], axis=0)
    spec = jnp.einsum("pfke,fje->pfkj", lead, cols, preferred_element_type=jnp.float32)
    return spec[:, :, None]


def solution(mesh):
    from jax.sharding import Mesh
    fine = Mesh(mesh.devices.reshape(4, 2, 4, 2, 4), ("zlo", "core", "drow", "zhi", "y"))
    placed = (P(None, None, ("drow", "zhi", "y"), ("zlo", "core")), P(None, ("zlo", "core")), P(), P())
    return jax.shard_map(
        local,
        mesh=fine,
        in_specs=placed,
        out_specs=P(None, None, "drow", ("zlo", "core"), ("zhi", "y")),
        check_vma=False,
    )
```

```python
import math

import jax
import jax.numpy as jnp
from jax import lax
from jax.experimental import pallas as pl
from jax.experimental.pallas import tpu as pltpu
from jax.sharding import PartitionSpec as P

DIRS = 512
FREQS = 8
GRID = 1024
NODE_TILE = 256


def unit_phasor(turn):
    quarter = GRID // 4
    shifted = (turn + quarter // 2) & (GRID - 1)
    quadrant = shifted >> 8
    offset = (shifted & (quarter - 1)) - quarter // 2
    x = offset.astype(jnp.float32) * (2.0 * math.pi / GRID)
    x2 = x * x
    s = x * (1.0 + x2 * (-1.0 / 6 + x2 * (1.0 / 120 + x2 * (-1.0 / 5040 + x2 * (1.0 / 362880)))))
    c = 1.0 + x2 * (-0.5 + x2 * (1.0 / 24 + x2 * (-1.0 / 720 + x2 * (1.0 / 40320))))
    odd = (quadrant & 1) == 1
    cos_mag = jnp.where(odd, s, c)
    sin_mag = jnp.where(odd, c, s)
    cos_neg = (quadrant == 1) | (quadrant == 2)
    sin_neg = quadrant >= 2
    return jnp.where(cos_neg, -cos_mag, cos_mag), jnp.where(sin_neg, -sin_mag, sin_mag)


def amp_kernel(proj_ref, spread_ref, resp_ref, out_ref):
    @pl.when(pl.program_id(0) == 0)
    def _():
        out_ref[...] = jnp.zeros_like(out_ref)

    proj = proj_ref[...]
    base_c, base_s = unit_phasor(proj & (GRID - 1))
    rows = resp_ref.shape[2]
    cos_f, sin_f = base_c, base_s
    for f in range(FREQS):
        if f > 0:
            cos_f, sin_f = (
                cos_f * base_c - sin_f * base_s,
                sin_f * base_c + cos_f * base_s,
            )
        spread = spread_ref[f : f + 1, :]
        load_re = (spread * cos_f).astype(jnp.bfloat16)
        load_im = (-spread * sin_f).astype(jnp.bfloat16)
        resp = resp_ref[:, f].reshape(2 * rows, resp_ref.shape[3])
        by_re = jnp.dot(resp, load_re, preferred_element_type=jnp.float32)
        by_im = jnp.dot(resp, load_im, preferred_element_type=jnp.float32)
        out_ref[f, :, :DIRS] += by_re[:rows] - by_im[rows:]
        out_ref[f, :, DIRS:] += by_im[:rows] + by_re[rows:]


def partial_amplitudes(freq_resp, project, spread):
    nodes = project.shape[0]
    rows = freq_resp.shape[2]
    return pl.pallas_call(
        amp_kernel,
        out_shape=jax.ShapeDtypeStruct((FREQS, rows, 2 * DIRS), jnp.float32),
        grid=(nodes // NODE_TILE,),
        in_specs=[
            pl.BlockSpec((NODE_TILE, DIRS), lambda j: (j, 0)),
            pl.BlockSpec((FREQS, DIRS), lambda j: (0, 0)),
            pl.BlockSpec((2, FREQS, rows, NODE_TILE), lambda j: (0, 0, 0, j)),
        ],
        out_specs=pl.BlockSpec((FREQS, rows, 2 * DIRS), lambda j: (0, 0, 0)),
        compiler_params=pltpu.CompilerParams(dimension_semantics=("arbitrary",)),
    )(project, spread, freq_resp)


def gather_cols(amplitudes):
    freqs, piece, width = amplitudes.shape
    mine = lax.all_gather(amplitudes, ("zlo", "drow"), axis=1)
    mine = mine.reshape(freqs, lax.axis_size("zlo"), -1, piece, width)
    theirs = lax.ppermute(mine, "core", perm=[(0, 1), (1, 0)])
    first = lax.axis_index("core") == 0
    pair = jnp.where(first, jnp.stack([mine, theirs], axis=2), jnp.stack([theirs, mine], axis=2))
    return pair.reshape(freqs, -1, width)


def gather_rows(amplitudes):
    count = lax.axis_size("zhi") * lax.axis_size("y")
    ahead = [amplitudes]
    for shift in range(1, count):
        ahead.append(
            lax.ppermute(
                amplitudes, ("zhi", "y"), perm=[(i, (i - shift) % count) for i in range(count)]
            )
        )
    stacked = jnp.stack(ahead, axis=1)
    rolled = jnp.roll(stacked, lax.axis_index(("zhi", "y")), axis=1)
    return rolled.reshape(stacked.shape[0], -1, stacked.shape[-1])


def local(freq_resp, node_coords, heading_steps, spectral_weights):
    project = (
        node_coords[0][:, None] * heading_steps[0][None, :]
        + node_coords[1][:, None] * heading_steps[1][None, :]
    )
    spread = jnp.sqrt(spectral_weights.astype(jnp.float32) / (64.0 * DIRS))
    partial_amp = partial_amplitudes(freq_resp, project, spread)
    amplitudes = lax.psum_scatter(partial_amp, ("zlo", "core"), scatter_dimension=1, tiled=True).astype(
        jnp.bfloat16
    )
    cols = gather_cols(amplitudes)
    rows = gather_rows(amplitudes)
    rows_im = jnp.concatenate([rows[..., DIRS:], -rows[..., :DIRS]], axis=-1)
    lead = jnp.stack([rows, rows_im], axis=0)
    spec = jnp.einsum("pfke,fje->pfkj", lead, cols, preferred_element_type=jnp.float32)
    return spec[:, :, None]


def solution(mesh):
    from jax.sharding import Mesh
    fine = Mesh(mesh.devices.reshape(4, 2, 4, 2, 4), ("zlo", "core", "drow", "zhi", "y"))
    placed = (P(None, None, ("drow", "zhi", "y"), ("zlo", "core")), P(None, ("zlo", "core")), P(), P())
    return jax.shard_map(
        local,
        mesh=fine,
        in_specs=placed,
        out_specs=P(None, None, "drow", ("zlo", "core"), ("zhi", "y")),
        check_vma=False,
    )
```

```python
import math

import jax
import jax.numpy as jnp
from jax import lax
from jax.experimental import pallas as pl
from jax.experimental.pallas import tpu as pltpu
from jax.sharding import PartitionSpec as P

DIRS = 512
FREQS = 8
GRID = 1024
NODE_TILE = 256


def unit_phasor(turn):
    quarter = GRID // 4
    shifted = (turn + quarter // 2) & (GRID - 1)
    quadrant = shifted >> 8
    offset = (shifted & (quarter - 1)) - quarter // 2
    x = offset.astype(jnp.float32) * (2.0 * math.pi / GRID)
    x2 = x * x
    s = x * (1.0 + x2 * (-1.0 / 6 + x2 * (1.0 / 120 + x2 * (-1.0 / 5040 + x2 * (1.0 / 362880)))))
    c = 1.0 + x2 * (-0.5 + x2 * (1.0 / 24 + x2 * (-1.0 / 720 + x2 * (1.0 / 40320))))
    odd = (quadrant & 1) == 1
    cos_mag = jnp.where(odd, s, c)
    sin_mag = jnp.where(odd, c, s)
    cos_neg = (quadrant == 1) | (quadrant == 2)
    sin_neg = quadrant >= 2
    return jnp.where(cos_neg, -cos_mag, cos_mag), jnp.where(sin_neg, -sin_mag, sin_mag)


def amp_kernel(proj_ref, spread_ref, resp_ref, out_ref):
    @pl.when(pl.program_id(0) == 0)
    def _():
        out_ref[...] = jnp.zeros_like(out_ref)

    proj = proj_ref[...]
    base_c, base_s = unit_phasor(proj & (GRID - 1))
    rows = resp_ref.shape[2]
    cos_f, sin_f = base_c, base_s
    for f in range(FREQS):
        if f > 0:
            cos_f, sin_f = (
                cos_f * base_c - sin_f * base_s,
                sin_f * base_c + cos_f * base_s,
            )
        spread = spread_ref[f : f + 1, :]
        load_re = (spread * cos_f).astype(jnp.bfloat16)
        load_im = (-spread * sin_f).astype(jnp.bfloat16)
        resp = resp_ref[:, f].reshape(2 * rows, resp_ref.shape[3])
        by_re = jnp.dot(resp, load_re, preferred_element_type=jnp.float32)
        by_im = jnp.dot(resp, load_im, preferred_element_type=jnp.float32)
        out_ref[f, :, :DIRS] += by_re[:rows] - by_im[rows:]
        out_ref[f, :, DIRS:] += by_im[:rows] + by_re[rows:]


def partial_amplitudes(freq_resp, project, spread):
    nodes = project.shape[0]
    rows = freq_resp.shape[2]
    return pl.pallas_call(
        amp_kernel,
        out_shape=jax.ShapeDtypeStruct((FREQS, rows, 2 * DIRS), jnp.float32),
        grid=(nodes // NODE_TILE,),
        in_specs=[
            pl.BlockSpec((NODE_TILE, DIRS), lambda j: (j, 0)),
            pl.BlockSpec((FREQS, DIRS), lambda j: (0, 0)),
            pl.BlockSpec((2, FREQS, rows, NODE_TILE), lambda j: (0, 0, 0, j)),
        ],
        out_specs=pl.BlockSpec((FREQS, rows, 2 * DIRS), lambda j: (0, 0, 0)),
        compiler_params=pltpu.CompilerParams(dimension_semantics=("arbitrary",)),
    )(project, spread, freq_resp)


def gather_by_permutes(piece, axis_name, count):
    ahead = [piece]
    for shift in range(1, count):
        ahead.append(
            lax.ppermute(piece, axis_name, perm=[(i, (i - shift) % count) for i in range(count)])
        )
    stacked = jnp.stack(ahead, axis=1)
    return jnp.roll(stacked, lax.axis_index(axis_name), axis=1)


def gather_cols(amplitudes):
    freqs, piece, width = amplitudes.shape
    along_z = gather_by_permutes(amplitudes, "zlo", lax.axis_size("zlo"))
    mine = lax.all_gather(along_z, "drow", axis=2)
    theirs = lax.ppermute(mine, "core", perm=[(0, 1), (1, 0)])
    first = lax.axis_index("core") == 0
    pair = jnp.where(first, jnp.stack([mine, theirs], axis=2), jnp.stack([theirs, mine], axis=2))
    return pair.reshape(freqs, -1, width)


def gather_rows(amplitudes):
    count = lax.axis_size("zhi") * lax.axis_size("y")
    rows = gather_by_permutes(amplitudes, ("zhi", "y"), count)
    return rows.reshape(amplitudes.shape[0], -1, amplitudes.shape[-1])


def local(freq_resp, node_coords, heading_steps, spectral_weights):
    project = (
        node_coords[0][:, None] * heading_steps[0][None, :]
        + node_coords[1][:, None] * heading_steps[1][None, :]
    )
    spread = jnp.sqrt(spectral_weights.astype(jnp.float32) / (64.0 * DIRS))
    partial_amp = partial_amplitudes(freq_resp, project, spread)
    amplitudes = lax.psum_scatter(partial_amp, ("zlo", "core"), scatter_dimension=1, tiled=True).astype(
        jnp.bfloat16
    )
    cols = gather_cols(amplitudes)
    rows = gather_rows(amplitudes)
    rows_im = jnp.concatenate([rows[..., DIRS:], -rows[..., :DIRS]], axis=-1)
    lead = jnp.stack([rows, rows_im], axis=0)
    spec = jnp.einsum("pfke,fje->pfkj", lead, cols, preferred_element_type=jnp.float32)
    return spec[:, :, None]


def solution(mesh):
    from jax.sharding import Mesh
    fine = Mesh(mesh.devices.reshape(4, 2, 4, 2, 4), ("zlo", "core", "drow", "zhi", "y"))
    placed = (P(None, None, ("drow", "zhi", "y"), ("zlo", "core")), P(None, ("zlo", "core")), P(), P())
    return jax.shard_map(
        local,
        mesh=fine,
        in_specs=placed,
        out_specs=P(None, None, "drow", ("zlo", "core"), ("zhi", "y")),
        check_vma=False,
    )
```

```python
import math

import jax
import jax.numpy as jnp
from jax import lax
from jax.experimental import pallas as pl
from jax.experimental.pallas import tpu as pltpu
from jax.sharding import PartitionSpec as P

DIRS = 512
FREQS = 8
GRID = 1024
NODE_TILE = 256


def unit_phasor(turn):
    quarter = GRID // 4
    shifted = (turn + quarter // 2) & (GRID - 1)
    quadrant = shifted >> 8
    offset = (shifted & (quarter - 1)) - quarter // 2
    x = offset.astype(jnp.float32) * (2.0 * math.pi / GRID)
    x2 = x * x
    s = x * (1.0 + x2 * (-1.0 / 6 + x2 * (1.0 / 120 + x2 * (-1.0 / 5040 + x2 * (1.0 / 362880)))))
    c = 1.0 + x2 * (-0.5 + x2 * (1.0 / 24 + x2 * (-1.0 / 720 + x2 * (1.0 / 40320))))
    odd = (quadrant & 1) == 1
    cos_mag = jnp.where(odd, s, c)
    sin_mag = jnp.where(odd, c, s)
    cos_neg = (quadrant == 1) | (quadrant == 2)
    sin_neg = quadrant >= 2
    return jnp.where(cos_neg, -cos_mag, cos_mag), jnp.where(sin_neg, -sin_mag, sin_mag)


def amp_kernel(proj_ref, spread_ref, resp_ref, out_ref):
    @pl.when(pl.program_id(0) == 0)
    def _():
        out_ref[...] = jnp.zeros_like(out_ref)

    proj = proj_ref[...]
    base_c, base_s = unit_phasor(proj & (GRID - 1))
    rows = resp_ref.shape[2]
    cos_f, sin_f = base_c, base_s
    for f in range(FREQS):
        if f > 0:
            cos_f, sin_f = (
                cos_f * base_c - sin_f * base_s,
                sin_f * base_c + cos_f * base_s,
            )
        spread = spread_ref[f : f + 1, :]
        load_re = (spread * cos_f).astype(jnp.bfloat16)
        load_im = (-spread * sin_f).astype(jnp.bfloat16)
        resp = resp_ref[:, f].reshape(2 * rows, resp_ref.shape[3])
        by_re = jnp.dot(resp, load_re, preferred_element_type=jnp.float32)
        by_im = jnp.dot(resp, load_im, preferred_element_type=jnp.float32)
        out_ref[f, :, :DIRS] += by_re[:rows] - by_im[rows:]
        out_ref[f, :, DIRS:] += by_im[:rows] + by_re[rows:]


def partial_amplitudes(freq_resp, project, spread):
    nodes = project.shape[0]
    rows = freq_resp.shape[2]
    return pl.pallas_call(
        amp_kernel,
        out_shape=jax.ShapeDtypeStruct((FREQS, rows, 2 * DIRS), jnp.float32),
        grid=(nodes // NODE_TILE,),
        in_specs=[
            pl.BlockSpec((NODE_TILE, DIRS), lambda j: (j, 0)),
            pl.BlockSpec((FREQS, DIRS), lambda j: (0, 0)),
            pl.BlockSpec((2, FREQS, rows, NODE_TILE), lambda j: (0, 0, 0, j)),
        ],
        out_specs=pl.BlockSpec((FREQS, rows, 2 * DIRS), lambda j: (0, 0, 0)),
        compiler_params=pltpu.CompilerParams(dimension_semantics=("arbitrary",)),
    )(project, spread, freq_resp)


def gather_cols(amplitudes):
    freqs, piece, width = amplitudes.shape
    along_z = lax.all_gather(amplitudes, "zlo", axis=1, tiled=True)
    along_z = along_z.reshape(freqs, -1, piece, width)
    mine = lax.all_gather(along_z, "drow", axis=2)
    theirs = lax.ppermute(mine, "core", perm=[(0, 1), (1, 0)])
    first = lax.axis_index("core") == 0
    pair = jnp.where(first, jnp.stack([mine, theirs], axis=2), jnp.stack([theirs, mine], axis=2))
    return pair.reshape(freqs, -1, width)


def gather_by_permutes(piece, axis_name, count):
    ahead = [piece]
    for shift in range(1, count):
        ahead.append(
            lax.ppermute(piece, axis_name, perm=[(i, (i - shift) % count) for i in range(count)])
        )
    stacked = jnp.stack(ahead, axis=1)
    return jnp.roll(stacked, lax.axis_index(axis_name), axis=1)


def gather_rows(amplitudes):
    freqs, piece, width = amplitudes.shape
    other = lax.ppermute(amplitudes, "zhi", perm=[(0, 1), (1, 0)])
    first = lax.axis_index("zhi") == 0
    pair = jnp.where(first, jnp.stack([amplitudes, other], 1), jnp.stack([other, amplitudes], 1))
    rows = gather_by_permutes(pair, "y", lax.axis_size("y"))
    return rows.transpose(0, 2, 1, 3, 4).reshape(freqs, -1, width)


def local(freq_resp, node_coords, heading_steps, spectral_weights):
    project = (
        node_coords[0][:, None] * heading_steps[0][None, :]
        + node_coords[1][:, None] * heading_steps[1][None, :]
    )
    spread = jnp.sqrt(spectral_weights.astype(jnp.float32) / (64.0 * DIRS))
    partial_amp = partial_amplitudes(freq_resp, project, spread)
    amplitudes = lax.psum_scatter(partial_amp, ("zlo", "core"), scatter_dimension=1, tiled=True).astype(
        jnp.bfloat16
    )
    cols = gather_cols(amplitudes)
    rows = gather_rows(amplitudes)
    rows_im = jnp.concatenate([rows[..., DIRS:], -rows[..., :DIRS]], axis=-1)
    lead = jnp.stack([rows, rows_im], axis=0)
    spec = jnp.einsum("pfke,fje->pfkj", lead, cols, preferred_element_type=jnp.float32)
    return spec[:, :, None]


def solution(mesh):
    from jax.sharding import Mesh
    fine = Mesh(mesh.devices.reshape(4, 2, 4, 2, 4), ("zlo", "core", "drow", "zhi", "y"))
    placed = (P(None, None, ("drow", "zhi", "y"), ("zlo", "core")), P(None, ("zlo", "core")), P(), P())
    return jax.shard_map(
        local,
        mesh=fine,
        in_specs=placed,
        out_specs=P(None, None, "drow", ("zlo", "core"), ("zhi", "y")),
        check_vma=False,
    )
```

```python
import math

import jax
import jax.numpy as jnp
from jax import lax
from jax.experimental import pallas as pl
from jax.experimental.pallas import tpu as pltpu
from jax.sharding import PartitionSpec as P

DIRS = 512
FREQS = 8
GRID = 1024
NODE_TILE = 256


def unit_phasor(turn):
    quarter = GRID // 4
    shifted = (turn + quarter // 2) & (GRID - 1)
    quadrant = shifted >> 8
    offset = (shifted & (quarter - 1)) - quarter // 2
    x = offset.astype(jnp.float32) * (2.0 * math.pi / GRID)
    x2 = x * x
    s = x * (1.0 + x2 * (-1.0 / 6 + x2 * (1.0 / 120 + x2 * (-1.0 / 5040 + x2 * (1.0 / 362880)))))
    c = 1.0 + x2 * (-0.5 + x2 * (1.0 / 24 + x2 * (-1.0 / 720 + x2 * (1.0 / 40320))))
    odd = (quadrant & 1) == 1
    cos_mag = jnp.where(odd, s, c)
    sin_mag = jnp.where(odd, c, s)
    cos_neg = (quadrant == 1) | (quadrant == 2)
    sin_neg = quadrant >= 2
    return jnp.where(cos_neg, -cos_mag, cos_mag), jnp.where(sin_neg, -sin_mag, sin_mag)


def amp_kernel(proj_ref, spread_ref, resp_ref, out_ref):
    @pl.when(pl.program_id(0) == 0)
    def _():
        out_ref[...] = jnp.zeros_like(out_ref)

    proj = proj_ref[...]
    base_c, base_s = unit_phasor(proj & (GRID - 1))
    rows = resp_ref.shape[2]
    cos_f, sin_f = base_c, base_s
    for f in range(FREQS):
        if f > 0:
            cos_f, sin_f = (
                cos_f * base_c - sin_f * base_s,
                sin_f * base_c + cos_f * base_s,
            )
        spread = spread_ref[f : f + 1, :]
        load_re = (spread * cos_f).astype(jnp.bfloat16)
        load_im = (-spread * sin_f).astype(jnp.bfloat16)
        resp = resp_ref[:, f].reshape(2 * rows, resp_ref.shape[3])
        by_re = jnp.dot(resp, load_re, preferred_element_type=jnp.float32)
        by_im = jnp.dot(resp, load_im, preferred_element_type=jnp.float32)
        out_ref[f, :, :DIRS] += by_re[:rows] - by_im[rows:]
        out_ref[f, :, DIRS:] += by_im[:rows] + by_re[rows:]


def partial_amplitudes(freq_resp, project, spread):
    nodes = project.shape[0]
    rows = freq_resp.shape[2]
    return pl.pallas_call(
        amp_kernel,
        out_shape=jax.ShapeDtypeStruct((FREQS, rows, 2 * DIRS), jnp.float32),
        grid=(nodes // NODE_TILE,),
        in_specs=[
            pl.BlockSpec((NODE_TILE, DIRS), lambda j: (j, 0)),
            pl.BlockSpec((FREQS, DIRS), lambda j: (0, 0)),
            pl.BlockSpec((2, FREQS, rows, NODE_TILE), lambda j: (0, 0, 0, j)),
        ],
        out_specs=pl.BlockSpec((FREQS, rows, 2 * DIRS), lambda j: (0, 0, 0)),
        compiler_params=pltpu.CompilerParams(dimension_semantics=("arbitrary",)),
    )(project, spread, freq_resp)


def gather_cols(along_z):
    freqs, width = along_z.shape[0], along_z.shape[-1]
    mine = lax.all_gather(along_z, "drow", axis=2)
    theirs = lax.ppermute(mine, "core", perm=[(0, 1), (1, 0)])
    first = lax.axis_index("core") == 0
    pair = jnp.where(first, jnp.stack([mine, theirs], axis=2), jnp.stack([theirs, mine], axis=2))
    return pair.reshape(freqs, -1, width)


def gather_rows(amplitudes):
    count = lax.axis_size("zhi") * lax.axis_size("y")
    ahead = [amplitudes]
    for shift in range(1, count):
        ahead.append(
            lax.ppermute(
                amplitudes, ("zhi", "y"), perm=[(i, (i - shift) % count) for i in range(count)]
            )
        )
    stacked = jnp.stack(ahead, axis=1)
    rolled = jnp.roll(stacked, lax.axis_index(("zhi", "y")), axis=1)
    return rolled.reshape(stacked.shape[0], -1, stacked.shape[-1])


def local(freq_resp, node_coords, heading_steps, spectral_weights):
    project = (
        node_coords[0][:, None] * heading_steps[0][None, :]
        + node_coords[1][:, None] * heading_steps[1][None, :]
    )
    spread = jnp.sqrt(spectral_weights.astype(jnp.float32) / (64.0 * DIRS))
    partial_amp = partial_amplitudes(freq_resp, project, spread)
    summed = lax.psum(partial_amp, ("zlo", "core")).astype(jnp.bfloat16)
    freqs, dofs, width = summed.shape
    zlo_count = lax.axis_size("zlo")
    split = summed.reshape(freqs, zlo_count, 2, dofs // (2 * zlo_count), width)
    along_z = lax.dynamic_index_in_dim(split, lax.axis_index("core"), axis=2, keepdims=False)
    amplitudes = lax.dynamic_index_in_dim(along_z, lax.axis_index("zlo"), axis=1, keepdims=False)
    cols = gather_cols(along_z)
    rows = gather_rows(amplitudes)
    rows_im = jnp.concatenate([rows[..., DIRS:], -rows[..., :DIRS]], axis=-1)
    lead = jnp.stack([rows, rows_im], axis=0)
    spec = jnp.einsum("pfke,fje->pfkj", lead, cols, preferred_element_type=jnp.float32)
    return spec[:, :, None]


def solution(mesh):
    from jax.sharding import Mesh
    fine = Mesh(mesh.devices.reshape(4, 2, 4, 2, 4), ("zlo", "core", "drow", "zhi", "y"))
    placed = (P(None, None, ("drow", "zhi", "y"), ("zlo", "core")), P(None, ("zlo", "core")), P(), P())
    return jax.shard_map(
        local,
        mesh=fine,
        in_specs=placed,
        out_specs=P(None, None, "drow", ("zlo", "core"), ("zhi", "y")),
        check_vma=False,
    )
```

```python
import math

import jax
import jax.numpy as jnp
from jax import lax
from jax.experimental import pallas as pl
from jax.experimental.pallas import tpu as pltpu
from jax.sharding import PartitionSpec as P

DIRS = 512
FREQS = 8
GRID = 1024
NODE_TILE = 256


def unit_phasor(turn):
    quarter = GRID // 4
    shifted = (turn + quarter // 2) & (GRID - 1)
    quadrant = shifted >> 8
    offset = (shifted & (quarter - 1)) - quarter // 2
    x = offset.astype(jnp.float32) * (2.0 * math.pi / GRID)
    x2 = x * x
    s = x * (1.0 + x2 * (-1.0 / 6 + x2 * (1.0 / 120 + x2 * (-1.0 / 5040 + x2 * (1.0 / 362880)))))
    c = 1.0 + x2 * (-0.5 + x2 * (1.0 / 24 + x2 * (-1.0 / 720 + x2 * (1.0 / 40320))))
    odd = (quadrant & 1) == 1
    cos_mag = jnp.where(odd, s, c)
    sin_mag = jnp.where(odd, c, s)
    cos_neg = (quadrant == 1) | (quadrant == 2)
    sin_neg = quadrant >= 2
    return jnp.where(cos_neg, -cos_mag, cos_mag), jnp.where(sin_neg, -sin_mag, sin_mag)


def amp_kernel(proj_ref, spread_ref, resp_ref, out_ref):
    @pl.when(pl.program_id(0) == 0)
    def _():
        out_ref[...] = jnp.zeros_like(out_ref)

    proj = proj_ref[...]
    base_c, base_s = unit_phasor(proj & (GRID - 1))
    rows = resp_ref.shape[2]
    cos_f, sin_f = base_c, base_s
    for f in range(FREQS):
        if f > 0:
            cos_f, sin_f = (
                cos_f * base_c - sin_f * base_s,
                sin_f * base_c + cos_f * base_s,
            )
        spread = spread_ref[f : f + 1, :]
        load_re = (spread * cos_f).astype(jnp.bfloat16)
        load_im = (-spread * sin_f).astype(jnp.bfloat16)
        resp = resp_ref[:, f].reshape(2 * rows, resp_ref.shape[3])
        by_re = jnp.dot(resp, load_re, preferred_element_type=jnp.float32)
        by_im = jnp.dot(resp, load_im, preferred_element_type=jnp.float32)
        out_ref[f, :, :DIRS] += by_re[:rows] - by_im[rows:]
        out_ref[f, :, DIRS:] += by_im[:rows] + by_re[rows:]


def partial_amplitudes(freq_resp, project, spread):
    nodes = project.shape[0]
    rows = freq_resp.shape[2]
    return pl.pallas_call(
        amp_kernel,
        out_shape=jax.ShapeDtypeStruct((FREQS, rows, 2 * DIRS), jnp.float32),
        grid=(nodes // NODE_TILE,),
        in_specs=[
            pl.BlockSpec((NODE_TILE, DIRS), lambda j: (j, 0)),
            pl.BlockSpec((FREQS, DIRS), lambda j: (0, 0)),
            pl.BlockSpec((2, FREQS, rows, NODE_TILE), lambda j: (0, 0, 0, j)),
        ],
        out_specs=pl.BlockSpec((FREQS, rows, 2 * DIRS), lambda j: (0, 0, 0)),
        compiler_params=pltpu.CompilerParams(dimension_semantics=("arbitrary",)),
    )(project, spread, freq_resp)


def gather_cols(amplitudes, rows):
    freqs, piece, width = amplitudes.shape
    along_z = lax.all_gather(amplitudes, "zlo", axis=1, tiled=True)
    along_z, rows = lax.optimization_barrier((along_z, rows))
    along_z = along_z.reshape(freqs, -1, piece, width)
    mine = lax.all_gather(along_z, "drow", axis=2)
    theirs = lax.ppermute(mine, "core", perm=[(0, 1), (1, 0)])
    first = lax.axis_index("core") == 0
    pair = jnp.where(first, jnp.stack([mine, theirs], axis=2), jnp.stack([theirs, mine], axis=2))
    return pair.reshape(freqs, -1, width), rows


def gather_rows(amplitudes):
    count = lax.axis_size("zhi") * lax.axis_size("y")
    freqs, piece, width = amplitudes.shape
    copies = jnp.broadcast_to(amplitudes[None], (count, freqs, piece, width))
    pieces = lax.all_to_all(copies, ("zhi", "y"), split_axis=0, concat_axis=0)
    return pieces.transpose(1, 0, 2, 3).reshape(freqs, -1, width)


def local(freq_resp, node_coords, heading_steps, spectral_weights):
    project = (
        node_coords[0][:, None] * heading_steps[0][None, :]
        + node_coords[1][:, None] * heading_steps[1][None, :]
    )
    spread = jnp.sqrt(spectral_weights.astype(jnp.float32) / (64.0 * DIRS))
    partial_amp = partial_amplitudes(freq_resp, project, spread)
    amplitudes = lax.psum_scatter(partial_amp, ("zlo", "core"), scatter_dimension=1, tiled=True).astype(
        jnp.bfloat16
    )
    cols, rows = gather_cols(amplitudes, gather_rows(amplitudes))
    rows_im = jnp.concatenate([rows[..., DIRS:], -rows[..., :DIRS]], axis=-1)
    lead = jnp.stack([rows, rows_im], axis=0)
    spec = jnp.einsum("pfke,fje->pfkj", lead, cols, preferred_element_type=jnp.float32)
    return spec[:, :, None]


def solution(mesh):
    from jax.sharding import Mesh
    fine = Mesh(mesh.devices.reshape(4, 2, 4, 2, 4), ("zlo", "core", "drow", "zhi", "y"))
    placed = (P(None, None, ("drow", "zhi", "y"), ("zlo", "core")), P(None, ("zlo", "core")), P(), P())
    return jax.shard_map(
        local,
        mesh=fine,
        in_specs=placed,
        out_specs=P(None, None, "drow", ("zlo", "core"), ("zhi", "y")),
        check_vma=False,
    )
```

```python
import math

import jax
import jax.numpy as jnp
from jax import lax
from jax.experimental import pallas as pl
from jax.experimental.pallas import tpu as pltpu
from jax.sharding import PartitionSpec as P

DIRS = 512
FREQS = 8
GRID = 1024
NODE_TILE = 256


def unit_phasor(turn):
    quarter = GRID // 4
    shifted = (turn + quarter // 2) & (GRID - 1)
    quadrant = shifted >> 8
    offset = (shifted & (quarter - 1)) - quarter // 2
    x = offset.astype(jnp.float32) * (2.0 * math.pi / GRID)
    x2 = x * x
    s = x * (1.0 + x2 * (-1.0 / 6 + x2 * (1.0 / 120 + x2 * (-1.0 / 5040 + x2 * (1.0 / 362880)))))
    c = 1.0 + x2 * (-0.5 + x2 * (1.0 / 24 + x2 * (-1.0 / 720 + x2 * (1.0 / 40320))))
    odd = (quadrant & 1) == 1
    cos_mag = jnp.where(odd, s, c)
    sin_mag = jnp.where(odd, c, s)
    cos_neg = (quadrant == 1) | (quadrant == 2)
    sin_neg = quadrant >= 2
    return jnp.where(cos_neg, -cos_mag, cos_mag), jnp.where(sin_neg, -sin_mag, sin_mag)


def amp_kernel(proj_ref, spread_ref, resp_ref, out_ref):
    @pl.when(pl.program_id(0) == 0)
    def _():
        out_ref[...] = jnp.zeros_like(out_ref)

    proj = proj_ref[...]
    base_c, base_s = unit_phasor(proj & (GRID - 1))
    rows = resp_ref.shape[2]
    cos_f, sin_f = base_c, base_s
    for f in range(FREQS):
        if f > 0:
            cos_f, sin_f = (
                cos_f * base_c - sin_f * base_s,
                sin_f * base_c + cos_f * base_s,
            )
        spread = spread_ref[f : f + 1, :]
        load_re = (spread * cos_f).astype(jnp.bfloat16)
        load_im = (-spread * sin_f).astype(jnp.bfloat16)
        resp = resp_ref[:, f].reshape(2 * rows, resp_ref.shape[3])
        by_re = jnp.dot(resp, load_re, preferred_element_type=jnp.float32)
        by_im = jnp.dot(resp, load_im, preferred_element_type=jnp.float32)
        out_ref[f, :, :DIRS] += by_re[:rows] - by_im[rows:]
        out_ref[f, :, DIRS:] += by_im[:rows] + by_re[rows:]


def partial_amplitudes(freq_resp, project, spread):
    nodes = project.shape[0]
    rows = freq_resp.shape[2]
    return pl.pallas_call(
        amp_kernel,
        out_shape=jax.ShapeDtypeStruct((FREQS, rows, 2 * DIRS), jnp.float32),
        grid=(nodes // NODE_TILE,),
        in_specs=[
            pl.BlockSpec((NODE_TILE, DIRS), lambda j: (j, 0)),
            pl.BlockSpec((FREQS, DIRS), lambda j: (0, 0)),
            pl.BlockSpec((2, FREQS, rows, NODE_TILE), lambda j: (0, 0, 0, j)),
        ],
        out_specs=pl.BlockSpec((FREQS, rows, 2 * DIRS), lambda j: (0, 0, 0)),
        compiler_params=pltpu.CompilerParams(dimension_semantics=("arbitrary",)),
    )(project, spread, freq_resp)


def gather_cols(amplitudes):
    freqs, piece, width = amplitudes.shape
    along_z = lax.all_gather(amplitudes, "zlo", axis=1, tiled=True)
    along_z, amplitudes = lax.optimization_barrier((along_z, amplitudes))
    rows = gather_rows(amplitudes)
    along_z = along_z.reshape(freqs, -1, piece, width)
    mine = lax.all_gather(along_z, "drow", axis=2)
    mine, rows = lax.optimization_barrier((mine, rows))
    theirs = lax.ppermute(mine, "core", perm=[(0, 1), (1, 0)])
    first = lax.axis_index("core") == 0
    pair = jnp.where(first, jnp.stack([mine, theirs], axis=2), jnp.stack([theirs, mine], axis=2))
    return pair.reshape(freqs, -1, width), rows


def gather_rows(amplitudes):
    count = lax.axis_size("zhi") * lax.axis_size("y")
    freqs, piece, width = amplitudes.shape
    copies = jnp.broadcast_to(amplitudes[None], (count, freqs, piece, width))
    pieces = lax.all_to_all(copies, ("zhi", "y"), split_axis=0, concat_axis=0)
    return pieces.transpose(1, 0, 2, 3).reshape(freqs, -1, width)


def local(freq_resp, node_coords, heading_steps, spectral_weights):
    project = (
        node_coords[0][:, None] * heading_steps[0][None, :]
        + node_coords[1][:, None] * heading_steps[1][None, :]
    )
    spread = jnp.sqrt(spectral_weights.astype(jnp.float32) / (64.0 * DIRS))
    partial_amp = partial_amplitudes(freq_resp, project, spread)
    amplitudes = lax.psum_scatter(partial_amp, ("zlo", "core"), scatter_dimension=1, tiled=True).astype(
        jnp.bfloat16
    )
    cols, rows = gather_cols(amplitudes)
    rows_im = jnp.concatenate([rows[..., DIRS:], -rows[..., :DIRS]], axis=-1)
    lead = jnp.stack([rows, rows_im], axis=0)
    spec = jnp.einsum("pfke,fje->pfkj", lead, cols, preferred_element_type=jnp.float32)
    return spec[:, :, None]


def solution(mesh):
    from jax.sharding import Mesh
    fine = Mesh(mesh.devices.reshape(4, 2, 4, 2, 4), ("zlo", "core", "drow", "zhi", "y"))
    placed = (P(None, None, ("drow", "zhi", "y"), ("zlo", "core")), P(None, ("zlo", "core")), P(), P())
    return jax.shard_map(
        local,
        mesh=fine,
        in_specs=placed,
        out_specs=P(None, None, "drow", ("zlo", "core"), ("zhi", "y")),
        check_vma=False,
    )
```

```python
import math

import jax
import jax.numpy as jnp
from jax import lax
from jax.experimental import pallas as pl
from jax.experimental.pallas import tpu as pltpu
from jax.sharding import PartitionSpec as P

DIRS = 512
FREQS = 8
GRID = 1024
NODE_TILE = 256


def unit_phasor(turn):
    quarter = GRID // 4
    shifted = (turn + quarter // 2) & (GRID - 1)
    quadrant = shifted >> 8
    offset = (shifted & (quarter - 1)) - quarter // 2
    x = offset.astype(jnp.float32) * (2.0 * math.pi / GRID)
    x2 = x * x
    s = x * (1.0 + x2 * (-1.0 / 6 + x2 * (1.0 / 120 + x2 * (-1.0 / 5040 + x2 * (1.0 / 362880)))))
    c = 1.0 + x2 * (-0.5 + x2 * (1.0 / 24 + x2 * (-1.0 / 720 + x2 * (1.0 / 40320))))
    odd = (quadrant & 1) == 1
    cos_mag = jnp.where(odd, s, c)
    sin_mag = jnp.where(odd, c, s)
    cos_neg = (quadrant == 1) | (quadrant == 2)
    sin_neg = quadrant >= 2
    return jnp.where(cos_neg, -cos_mag, cos_mag), jnp.where(sin_neg, -sin_mag, sin_mag)


def amp_kernel(proj_ref, spread_ref, resp_ref, out_ref):
    @pl.when(pl.program_id(0) == 0)
    def _():
        out_ref[...] = jnp.zeros_like(out_ref)

    proj = proj_ref[...]
    base_c, base_s = unit_phasor(proj & (GRID - 1))
    rows = resp_ref.shape[2]
    cos_f, sin_f = base_c, base_s
    for f in range(FREQS):
        if f > 0:
            cos_f, sin_f = (
                cos_f * base_c - sin_f * base_s,
                sin_f * base_c + cos_f * base_s,
            )
        spread = spread_ref[f : f + 1, :]
        load_re = (spread * cos_f).astype(jnp.bfloat16)
        load_im = (-spread * sin_f).astype(jnp.bfloat16)
        resp = resp_ref[:, f].reshape(2 * rows, resp_ref.shape[3])
        by_re = jnp.dot(resp, load_re, preferred_element_type=jnp.float32)
        by_im = jnp.dot(resp, load_im, preferred_element_type=jnp.float32)
        out_ref[f, :, :DIRS] += by_re[:rows] - by_im[rows:]
        out_ref[f, :, DIRS:] += by_im[:rows] + by_re[rows:]


def partial_amplitudes(freq_resp, project, spread):
    nodes = project.shape[0]
    rows = freq_resp.shape[2]
    return pl.pallas_call(
        amp_kernel,
        out_shape=jax.ShapeDtypeStruct((FREQS, rows, 2 * DIRS), jnp.float32),
        grid=(nodes // NODE_TILE,),
        in_specs=[
            pl.BlockSpec((NODE_TILE, DIRS), lambda j: (j, 0)),
            pl.BlockSpec((FREQS, DIRS), lambda j: (0, 0)),
            pl.BlockSpec((2, FREQS, rows, NODE_TILE), lambda j: (0, 0, 0, j)),
        ],
        out_specs=pl.BlockSpec((FREQS, rows, 2 * DIRS), lambda j: (0, 0, 0)),
        compiler_params=pltpu.CompilerParams(dimension_semantics=("arbitrary",)),
    )(project, spread, freq_resp)


def gather_cols(amplitudes):
    freqs, piece, width = amplitudes.shape
    along_z = lax.all_gather(amplitudes, "zlo", axis=1, tiled=True)
    along_z, amplitudes = lax.optimization_barrier((along_z, amplitudes))
    rows = gather_rows(amplitudes)
    along_z = along_z.reshape(freqs, -1, piece, width)
    mine = lax.all_gather(along_z, "drow", axis=0)
    mine, rows = lax.optimization_barrier((mine, rows))
    theirs = lax.ppermute(mine, "core", perm=[(0, 1), (1, 0)])
    return mine, theirs, rows


def spec_kernel(core_ref, rows_ref, mine_ref, theirs_ref, out_ref):
    rows = rows_ref[0]
    first = core_ref[0] == 0
    contract = (((1,), (1,)), ((), ()))

    def dot(a, b):
        return lax.dot_general(a, b, contract, preferred_element_type=jnp.float32)

    zlo_count = mine_ref.shape[2]
    block = 2 * mine_ref.shape[0] * mine_ref.shape[3]
    for z in range(zlo_count):
        own = mine_ref[:, 0, z].reshape(-1, mine_ref.shape[-1])
        other = theirs_ref[:, 0, z].reshape(-1, mine_ref.shape[-1])
        cols = jnp.where(
            first, jnp.concatenate([own, other], axis=0), jnp.concatenate([other, own], axis=0)
        )
        out_ref[0, 0, :, z * block : (z + 1) * block] = dot(rows, cols)
        out_ref[1, 0, :, z * block : (z + 1) * block] = dot(rows[:, DIRS:], cols[:, :DIRS]) - dot(
            rows[:, :DIRS], cols[:, DIRS:]
        )


def cross_spectra(rows, mine, theirs):
    freqs, row_count, width = rows.shape
    col_count = 2 * mine.shape[0] * mine.shape[2] * mine.shape[3]
    core = lax.axis_index("core").astype(jnp.int32).reshape(1)
    col_spec = pl.BlockSpec((mine.shape[0], 1) + mine.shape[2:], lambda f: (0, f, 0, 0, 0))
    return pl.pallas_call(
        spec_kernel,
        out_shape=jax.ShapeDtypeStruct((2, freqs, row_count, col_count), jnp.float32),
        grid=(freqs,),
        in_specs=[
            pl.BlockSpec(memory_space=pltpu.SMEM),
            pl.BlockSpec((1, row_count, width), lambda f: (f, 0, 0)),
            col_spec,
            col_spec,
        ],
        out_specs=pl.BlockSpec((2, 1, row_count, col_count), lambda f: (0, f, 0, 0)),
        compiler_params=pltpu.CompilerParams(dimension_semantics=("arbitrary",)),
    )(core, rows, mine, theirs)


def gather_rows(amplitudes):
    count = lax.axis_size("zhi") * lax.axis_size("y")
    freqs, piece, width = amplitudes.shape
    copies = jnp.broadcast_to(amplitudes[None], (count, freqs, piece, width))
    pieces = lax.all_to_all(copies, ("zhi", "y"), split_axis=0, concat_axis=0)
    return pieces.transpose(1, 0, 2, 3).reshape(freqs, -1, width)


def local(freq_resp, node_coords, heading_steps, spectral_weights):
    project = (
        node_coords[0][:, None] * heading_steps[0][None, :]
        + node_coords[1][:, None] * heading_steps[1][None, :]
    )
    spread = jnp.sqrt(spectral_weights.astype(jnp.float32) / (64.0 * DIRS))
    partial_amp = partial_amplitudes(freq_resp, project, spread)
    amplitudes = lax.psum_scatter(partial_amp, ("zlo", "core"), scatter_dimension=1, tiled=True).astype(
        jnp.bfloat16
    )
    mine, theirs, rows = gather_cols(amplitudes)
    return cross_spectra(rows, mine, theirs)[:, :, None]


def solution(mesh):
    from jax.sharding import Mesh
    fine = Mesh(mesh.devices.reshape(4, 2, 4, 2, 4), ("zlo", "core", "drow", "zhi", "y"))
    placed = (P(None, None, ("drow", "zhi", "y"), ("zlo", "core")), P(None, ("zlo", "core")), P(), P())
    return jax.shard_map(
        local,
        mesh=fine,
        in_specs=placed,
        out_specs=P(None, None, "drow", ("zlo", "core"), ("zhi", "y")),
        check_vma=False,
    )
```

```python
import math

import jax
import jax.numpy as jnp
from jax import lax
from jax.experimental import pallas as pl
from jax.experimental.pallas import tpu as pltpu
from jax.sharding import PartitionSpec as P

DIRS = 512
FREQS = 8
GRID = 1024
NODE_TILE = 256


def unit_phasor(turn):
    quarter = GRID // 4
    shifted = (turn + quarter // 2) & (GRID - 1)
    quadrant = shifted >> 8
    offset = (shifted & (quarter - 1)) - quarter // 2
    x = offset.astype(jnp.float32) * (2.0 * math.pi / GRID)
    x2 = x * x
    s = x * (1.0 + x2 * (-1.0 / 6 + x2 * (1.0 / 120 + x2 * (-1.0 / 5040 + x2 * (1.0 / 362880)))))
    c = 1.0 + x2 * (-0.5 + x2 * (1.0 / 24 + x2 * (-1.0 / 720 + x2 * (1.0 / 40320))))
    odd = (quadrant & 1) == 1
    cos_mag = jnp.where(odd, s, c)
    sin_mag = jnp.where(odd, c, s)
    cos_neg = (quadrant == 1) | (quadrant == 2)
    sin_neg = quadrant >= 2
    return jnp.where(cos_neg, -cos_mag, cos_mag), jnp.where(sin_neg, -sin_mag, sin_mag)


def amp_kernel(proj_ref, spread_ref, resp_ref, out_ref):
    @pl.when(pl.program_id(0) == 0)
    def _():
        out_ref[...] = jnp.zeros_like(out_ref)

    proj = proj_ref[...]
    base_c, base_s = unit_phasor(proj & (GRID - 1))
    rows = resp_ref.shape[2]
    cos_f, sin_f = base_c, base_s
    for f in range(FREQS):
        if f > 0:
            cos_f, sin_f = (
                cos_f * base_c - sin_f * base_s,
                sin_f * base_c + cos_f * base_s,
            )
        spread = spread_ref[f : f + 1, :]
        load_re = (spread * cos_f).astype(jnp.bfloat16)
        load_im = (-spread * sin_f).astype(jnp.bfloat16)
        resp = resp_ref[:, f].reshape(2 * rows, resp_ref.shape[3])
        by_re = jnp.dot(resp, load_re, preferred_element_type=jnp.float32)
        by_im = jnp.dot(resp, load_im, preferred_element_type=jnp.float32)
        out_ref[f, :, :DIRS] += by_re[:rows] - by_im[rows:]
        out_ref[f, :, DIRS:] += by_im[:rows] + by_re[rows:]


def partial_amplitudes(freq_resp, project, spread):
    nodes = project.shape[0]
    rows = freq_resp.shape[2]
    return pl.pallas_call(
        amp_kernel,
        out_shape=jax.ShapeDtypeStruct((FREQS, rows, 2 * DIRS), jnp.float32),
        grid=(nodes // NODE_TILE,),
        in_specs=[
            pl.BlockSpec((NODE_TILE, DIRS), lambda j: (j, 0)),
            pl.BlockSpec((FREQS, DIRS), lambda j: (0, 0)),
            pl.BlockSpec((2, FREQS, rows, NODE_TILE), lambda j: (0, 0, 0, j)),
        ],
        out_specs=pl.BlockSpec((FREQS, rows, 2 * DIRS), lambda j: (0, 0, 0)),
        compiler_params=pltpu.CompilerParams(dimension_semantics=("arbitrary",)),
    )(project, spread, freq_resp)


def gather_cols(amplitudes):
    freqs, piece, width = amplitudes.shape
    along_z = gather_by_all_to_all(amplitudes, "zlo", lax.axis_size("zlo"))
    along_z, amplitudes = lax.optimization_barrier((along_z, amplitudes))
    rows = gather_rows(amplitudes)
    mine = lax.all_gather(along_z, "drow", axis=0)
    mine, rows = lax.optimization_barrier((mine, rows))
    theirs = lax.ppermute(mine, "core", perm=[(0, 1), (1, 0)])
    return mine, theirs, rows


def spec_kernel(core_ref, rows_ref, mine_ref, theirs_ref, out_ref):
    rows = rows_ref[0]
    first = core_ref[0] == 0
    contract = (((1,), (1,)), ((), ()))

    def dot(a, b):
        return lax.dot_general(a, b, contract, preferred_element_type=jnp.float32)

    zlo_count = mine_ref.shape[1]
    block = 2 * mine_ref.shape[0] * mine_ref.shape[3]
    for z in range(zlo_count):
        own = mine_ref[:, z, 0].reshape(-1, mine_ref.shape[-1])
        other = theirs_ref[:, z, 0].reshape(-1, mine_ref.shape[-1])
        cols = jnp.where(
            first, jnp.concatenate([own, other], axis=0), jnp.concatenate([other, own], axis=0)
        )
        out_ref[0, 0, :, z * block : (z + 1) * block] = dot(rows, cols)
        out_ref[1, 0, :, z * block : (z + 1) * block] = dot(rows[:, DIRS:], cols[:, :DIRS]) - dot(
            rows[:, :DIRS], cols[:, DIRS:]
        )


def cross_spectra(rows, mine, theirs):
    freqs, row_count, width = rows.shape
    col_count = 2 * mine.shape[0] * mine.shape[1] * mine.shape[3]
    core = lax.axis_index("core").astype(jnp.int32).reshape(1)
    col_spec = pl.BlockSpec(mine.shape[:2] + (1,) + mine.shape[3:], lambda f: (0, 0, f, 0, 0))
    return pl.pallas_call(
        spec_kernel,
        out_shape=jax.ShapeDtypeStruct((2, freqs, row_count, col_count), jnp.float32),
        grid=(freqs,),
        in_specs=[
            pl.BlockSpec(memory_space=pltpu.SMEM),
            pl.BlockSpec((1, row_count, width), lambda f: (f, 0, 0)),
            col_spec,
            col_spec,
        ],
        out_specs=pl.BlockSpec((2, 1, row_count, col_count), lambda f: (0, f, 0, 0)),
        compiler_params=pltpu.CompilerParams(dimension_semantics=("arbitrary",)),
    )(core, rows, mine, theirs)


def gather_by_all_to_all(piece, axis_name, count):
    copies = jnp.broadcast_to(piece[None], (count,) + piece.shape)
    return lax.all_to_all(copies, axis_name, split_axis=0, concat_axis=0)


def gather_rows(amplitudes):
    count = lax.axis_size("zhi") * lax.axis_size("y")
    freqs, piece, width = amplitudes.shape
    pieces = gather_by_all_to_all(amplitudes, ("zhi", "y"), count)
    return pieces.transpose(1, 0, 2, 3).reshape(freqs, -1, width)


def local(freq_resp, node_coords, heading_steps, spectral_weights):
    project = (
        node_coords[0][:, None] * heading_steps[0][None, :]
        + node_coords[1][:, None] * heading_steps[1][None, :]
    )
    spread = jnp.sqrt(spectral_weights.astype(jnp.float32) / (64.0 * DIRS))
    partial_amp = partial_amplitudes(freq_resp, project, spread)
    amplitudes = lax.psum_scatter(partial_amp, ("zlo", "core"), scatter_dimension=1, tiled=True).astype(
        jnp.bfloat16
    )
    mine, theirs, rows = gather_cols(amplitudes)
    return cross_spectra(rows, mine, theirs)[:, :, None]


def solution(mesh):
    from jax.sharding import Mesh
    fine = Mesh(mesh.devices.reshape(4, 2, 4, 2, 4), ("zlo", "core", "drow", "zhi", "y"))
    placed = (P(None, None, ("drow", "zhi", "y"), ("zlo", "core")), P(None, ("zlo", "core")), P(), P())
    return jax.shard_map(
        local,
        mesh=fine,
        in_specs=placed,
        out_specs=P(None, None, "drow", ("zlo", "core"), ("zhi", "y")),
        check_vma=False,
    )
```

```python
import math

import jax
import jax.numpy as jnp
from jax import lax
from jax.experimental import pallas as pl
from jax.experimental.pallas import tpu as pltpu
from jax.sharding import PartitionSpec as P

DIRS = 512
FREQS = 8
GRID = 1024
NODE_TILE = 256


def unit_phasor(turn):
    quarter = GRID // 4
    shifted = (turn + quarter // 2) & (GRID - 1)
    quadrant = shifted >> 8
    offset = (shifted & (quarter - 1)) - quarter // 2
    x = offset.astype(jnp.float32) * (2.0 * math.pi / GRID)
    x2 = x * x
    s = x * (1.0 + x2 * (-1.0 / 6 + x2 * (1.0 / 120 + x2 * (-1.0 / 5040 + x2 * (1.0 / 362880)))))
    c = 1.0 + x2 * (-0.5 + x2 * (1.0 / 24 + x2 * (-1.0 / 720 + x2 * (1.0 / 40320))))
    odd = (quadrant & 1) == 1
    cos_mag = jnp.where(odd, s, c)
    sin_mag = jnp.where(odd, c, s)
    cos_neg = (quadrant == 1) | (quadrant == 2)
    sin_neg = quadrant >= 2
    return jnp.where(cos_neg, -cos_mag, cos_mag), jnp.where(sin_neg, -sin_mag, sin_mag)


def amp_kernel(proj_ref, spread_ref, resp_ref, out_ref):
    @pl.when(pl.program_id(0) == 0)
    def _():
        out_ref[...] = jnp.zeros_like(out_ref)

    proj = proj_ref[...]
    base_c, base_s = unit_phasor(proj & (GRID - 1))
    rows = resp_ref.shape[2]
    cos_f, sin_f = base_c, base_s
    for f in range(FREQS):
        if f > 0:
            cos_f, sin_f = (
                cos_f * base_c - sin_f * base_s,
                sin_f * base_c + cos_f * base_s,
            )
        spread = spread_ref[f : f + 1, :]
        load_re = (spread * cos_f).astype(jnp.bfloat16)
        load_im = (-spread * sin_f).astype(jnp.bfloat16)
        resp = resp_ref[:, f].reshape(2 * rows, resp_ref.shape[3])
        by_re = jnp.dot(resp, load_re, preferred_element_type=jnp.float32)
        by_im = jnp.dot(resp, load_im, preferred_element_type=jnp.float32)
        out_ref[f, :, :DIRS] += by_re[:rows] - by_im[rows:]
        out_ref[f, :, DIRS:] += by_im[:rows] + by_re[rows:]


def partial_amplitudes(freq_resp, project, spread):
    nodes = project.shape[0]
    rows = freq_resp.shape[2]
    return pl.pallas_call(
        amp_kernel,
        out_shape=jax.ShapeDtypeStruct((FREQS, rows, 2 * DIRS), jnp.float32),
        grid=(nodes // NODE_TILE,),
        in_specs=[
            pl.BlockSpec((NODE_TILE, DIRS), lambda j: (j, 0)),
            pl.BlockSpec((FREQS, DIRS), lambda j: (0, 0)),
            pl.BlockSpec((2, FREQS, rows, NODE_TILE), lambda j: (0, 0, 0, j)),
        ],
        out_specs=pl.BlockSpec((FREQS, rows, 2 * DIRS), lambda j: (0, 0, 0)),
        compiler_params=pltpu.CompilerParams(dimension_semantics=("arbitrary",)),
    )(project, spread, freq_resp)


def gather_cols(amplitudes):
    freqs, piece, width = amplitudes.shape
    along_z = gather_by_all_to_all(amplitudes, "zlo", lax.axis_size("zlo"))
    along_z, amplitudes = lax.optimization_barrier((along_z, amplitudes))
    rows = gather_rows(amplitudes)
    mine = lax.all_gather(along_z, "drow", axis=0)
    mine, rows = lax.optimization_barrier((mine, rows))
    theirs = lax.ppermute(mine, "core", perm=[(0, 1), (1, 0)])
    return mine, theirs, rows


def spec_kernel(core_ref, rows_ref, mine_ref, theirs_ref, out_ref):
    rows = rows_ref[0]
    rows_im = jnp.concatenate([rows[:, DIRS:], -rows[:, :DIRS]], axis=1)
    first = core_ref[0] == 0
    contract = (((1,), (1,)), ((), ()))

    def dot(a, b):
        return lax.dot_general(a, b, contract, preferred_element_type=jnp.float32)

    zlo_count = mine_ref.shape[1]
    block = 2 * mine_ref.shape[0] * mine_ref.shape[3]
    for z in range(zlo_count):
        own = mine_ref[:, z, 0].reshape(-1, mine_ref.shape[-1])
        other = theirs_ref[:, z, 0].reshape(-1, mine_ref.shape[-1])
        cols = jnp.where(
            first, jnp.concatenate([own, other], axis=0), jnp.concatenate([other, own], axis=0)
        )
        out_ref[0, 0, :, z * block : (z + 1) * block] = dot(rows, cols)
        out_ref[1, 0, :, z * block : (z + 1) * block] = dot(rows_im, cols)


def cross_spectra(rows, mine, theirs):
    freqs, row_count, width = rows.shape
    col_count = 2 * mine.shape[0] * mine.shape[1] * mine.shape[3]
    core = lax.axis_index("core").astype(jnp.int32).reshape(1)
    col_spec = pl.BlockSpec(mine.shape[:2] + (1,) + mine.shape[3:], lambda f: (0, 0, f, 0, 0))
    return pl.pallas_call(
        spec_kernel,
        out_shape=jax.ShapeDtypeStruct((2, freqs, row_count, col_count), jnp.float32),
        grid=(freqs,),
        in_specs=[
            pl.BlockSpec(memory_space=pltpu.SMEM),
            pl.BlockSpec((1, row_count, width), lambda f: (f, 0, 0)),
            col_spec,
            col_spec,
        ],
        out_specs=pl.BlockSpec((2, 1, row_count, col_count), lambda f: (0, f, 0, 0)),
        compiler_params=pltpu.CompilerParams(dimension_semantics=("arbitrary",)),
    )(core, rows, mine, theirs)


def gather_by_all_to_all(piece, axis_name, count):
    copies = jnp.broadcast_to(piece[None], (count,) + piece.shape)
    return lax.all_to_all(copies, axis_name, split_axis=0, concat_axis=0)


def gather_rows(amplitudes):
    count = lax.axis_size("zhi") * lax.axis_size("y")
    freqs, piece, width = amplitudes.shape
    pieces = gather_by_all_to_all(amplitudes, ("zhi", "y"), count)
    return pieces.transpose(1, 0, 2, 3).reshape(freqs, -1, width)


def local(freq_resp, node_coords, heading_steps, spectral_weights):
    project = (
        node_coords[0][:, None] * heading_steps[0][None, :]
        + node_coords[1][:, None] * heading_steps[1][None, :]
    )
    spread = jnp.sqrt(spectral_weights.astype(jnp.float32) / (64.0 * DIRS))
    partial_amp = partial_amplitudes(freq_resp, project, spread)
    amplitudes = lax.psum_scatter(partial_amp, ("zlo", "core"), scatter_dimension=1, tiled=True).astype(
        jnp.bfloat16
    )
    mine, theirs, rows = gather_cols(amplitudes)
    return cross_spectra(rows, mine, theirs)[:, :, None]


def solution(mesh):
    from jax.sharding import Mesh
    fine = Mesh(mesh.devices.reshape(4, 2, 4, 2, 4), ("zlo", "core", "drow", "zhi", "y"))
    placed = (P(None, None, ("drow", "zhi", "y"), ("zlo", "core")), P(None, ("zlo", "core")), P(), P())
    return jax.shard_map(
        local,
        mesh=fine,
        in_specs=placed,
        out_specs=P(None, None, "drow", ("zlo", "core"), ("zhi", "y")),
        check_vma=False,
    )
```

```python
import math

import jax
import jax.numpy as jnp
from jax import lax
from jax.experimental import pallas as pl
from jax.experimental.pallas import tpu as pltpu
from jax.sharding import PartitionSpec as P

DIRS = 512
FREQS = 8
GRID = 1024
NODE_TILE = 256


def unit_phasor(turn):
    quarter = GRID // 4
    shifted = (turn + quarter // 2) & (GRID - 1)
    quadrant = shifted >> 8
    offset = (shifted & (quarter - 1)) - quarter // 2
    x = offset.astype(jnp.float32) * (2.0 * math.pi / GRID)
    x2 = x * x
    s = x * (1.0 + x2 * (-1.0 / 6 + x2 * (1.0 / 120 + x2 * (-1.0 / 5040 + x2 * (1.0 / 362880)))))
    c = 1.0 + x2 * (-0.5 + x2 * (1.0 / 24 + x2 * (-1.0 / 720 + x2 * (1.0 / 40320))))
    odd = (quadrant & 1) == 1
    cos_mag = jnp.where(odd, s, c)
    sin_mag = jnp.where(odd, c, s)
    cos_neg = (quadrant == 1) | (quadrant == 2)
    sin_neg = quadrant >= 2
    return jnp.where(cos_neg, -cos_mag, cos_mag), jnp.where(sin_neg, -sin_mag, sin_mag)


def amp_kernel(proj_ref, spread_ref, resp_ref, out_ref):
    @pl.when(pl.program_id(0) == 0)
    def _():
        out_ref[...] = jnp.zeros_like(out_ref)

    proj = proj_ref[...]
    base_c, base_s = unit_phasor(proj & (GRID - 1))
    rows = resp_ref.shape[2]
    cos_f, sin_f = base_c, base_s
    for f in range(FREQS):
        if f > 0:
            cos_f, sin_f = (
                cos_f * base_c - sin_f * base_s,
                sin_f * base_c + cos_f * base_s,
            )
        spread = spread_ref[f : f + 1, :]
        load_re = (spread * cos_f).astype(jnp.bfloat16)
        load_im = (-spread * sin_f).astype(jnp.bfloat16)
        resp = resp_ref[:, f].reshape(2 * rows, resp_ref.shape[3])
        by_re = jnp.dot(resp, load_re, preferred_element_type=jnp.float32)
        by_im = jnp.dot(resp, load_im, preferred_element_type=jnp.float32)
        out_ref[f, :, :DIRS] += by_re[:rows] - by_im[rows:]
        out_ref[f, :, DIRS:] += by_im[:rows] + by_re[rows:]


def partial_amplitudes(freq_resp, project, spread):
    nodes = project.shape[0]
    rows = freq_resp.shape[2]
    return pl.pallas_call(
        amp_kernel,
        out_shape=jax.ShapeDtypeStruct((FREQS, rows, 2 * DIRS), jnp.float32),
        grid=(nodes // NODE_TILE,),
        in_specs=[
            pl.BlockSpec((NODE_TILE, DIRS), lambda j: (j, 0)),
            pl.BlockSpec((FREQS, DIRS), lambda j: (0, 0)),
            pl.BlockSpec((2, FREQS, rows, NODE_TILE), lambda j: (0, 0, 0, j)),
        ],
        out_specs=pl.BlockSpec((FREQS, rows, 2 * DIRS), lambda j: (0, 0, 0)),
        compiler_params=pltpu.CompilerParams(dimension_semantics=("arbitrary",)),
    )(project, spread, freq_resp)


def gather_cols(amplitudes):
    freqs, piece, width = amplitudes.shape
    along_z = gather_by_permutes(amplitudes, "zlo", lax.axis_size("zlo"))
    along_z, amplitudes = lax.optimization_barrier((along_z, amplitudes))
    rows = gather_rows(amplitudes)
    mine = lax.all_gather(along_z, "drow", axis=0)
    mine, rows = lax.optimization_barrier((mine, rows))
    theirs = lax.ppermute(mine, "core", perm=[(0, 1), (1, 0)])
    return mine, theirs, rows


def spec_kernel(core_ref, rows_ref, mine_ref, theirs_ref, out_ref):
    rows = rows_ref[0]
    rows_im = jnp.concatenate([rows[:, DIRS:], -rows[:, :DIRS]], axis=1)
    first = core_ref[0] == 0
    contract = (((1,), (1,)), ((), ()))

    def dot(a, b):
        return lax.dot_general(a, b, contract, preferred_element_type=jnp.float32)

    zlo_count = mine_ref.shape[1]
    block = 2 * mine_ref.shape[0] * mine_ref.shape[3]
    for z in range(zlo_count):
        own = mine_ref[:, z, 0].reshape(-1, mine_ref.shape[-1])
        other = theirs_ref[:, z, 0].reshape(-1, mine_ref.shape[-1])
        cols = jnp.where(
            first, jnp.concatenate([own, other], axis=0), jnp.concatenate([other, own], axis=0)
        )
        out_ref[0, 0, :, z * block : (z + 1) * block] = dot(rows, cols)
        out_ref[1, 0, :, z * block : (z + 1) * block] = dot(rows_im, cols)


def cross_spectra(rows, mine, theirs):
    freqs, row_count, width = rows.shape
    col_count = 2 * mine.shape[0] * mine.shape[1] * mine.shape[3]
    core = lax.axis_index("core").astype(jnp.int32).reshape(1)
    col_spec = pl.BlockSpec(mine.shape[:2] + (1,) + mine.shape[3:], lambda f: (0, 0, f, 0, 0))
    return pl.pallas_call(
        spec_kernel,
        out_shape=jax.ShapeDtypeStruct((2, freqs, row_count, col_count), jnp.float32),
        grid=(freqs,),
        in_specs=[
            pl.BlockSpec(memory_space=pltpu.SMEM),
            pl.BlockSpec((1, row_count, width), lambda f: (f, 0, 0)),
            col_spec,
            col_spec,
        ],
        out_specs=pl.BlockSpec((2, 1, row_count, col_count), lambda f: (0, f, 0, 0)),
        compiler_params=pltpu.CompilerParams(dimension_semantics=("arbitrary",)),
    )(core, rows, mine, theirs)


def gather_by_permutes(piece, axis_name, count):
    ahead = [piece]
    for shift in range(1, count):
        ahead.append(
            lax.ppermute(piece, axis_name, perm=[(i, (i - shift) % count) for i in range(count)])
        )
    return jnp.roll(jnp.stack(ahead), lax.axis_index(axis_name), axis=0)


def gather_by_all_to_all(piece, axis_name, count):
    copies = jnp.broadcast_to(piece[None], (count,) + piece.shape)
    return lax.all_to_all(copies, axis_name, split_axis=0, concat_axis=0)


def gather_rows(amplitudes):
    count = lax.axis_size("zhi") * lax.axis_size("y")
    freqs, piece, width = amplitudes.shape
    pieces = gather_by_all_to_all(amplitudes, ("zhi", "y"), count)
    return pieces.transpose(1, 0, 2, 3).reshape(freqs, -1, width)


def local(freq_resp, node_coords, heading_steps, spectral_weights):
    project = (
        node_coords[0][:, None] * heading_steps[0][None, :]
        + node_coords[1][:, None] * heading_steps[1][None, :]
    )
    spread = jnp.sqrt(spectral_weights.astype(jnp.float32) / (64.0 * DIRS))
    partial_amp = partial_amplitudes(freq_resp, project, spread)
    amplitudes = lax.psum_scatter(partial_amp, ("zlo", "core"), scatter_dimension=1, tiled=True).astype(
        jnp.bfloat16
    )
    mine, theirs, rows = gather_cols(amplitudes)
    return cross_spectra(rows, mine, theirs)[:, :, None]


def solution(mesh):
    from jax.sharding import Mesh
    fine = Mesh(mesh.devices.reshape(4, 2, 4, 2, 4), ("zlo", "core", "drow", "zhi", "y"))
    placed = (P(None, None, ("drow", "zhi", "y"), ("zlo", "core")), P(None, ("zlo", "core")), P(), P())
    return jax.shard_map(
        local,
        mesh=fine,
        in_specs=placed,
        out_specs=P(None, None, "drow", ("zlo", "core"), ("zhi", "y")),
        check_vma=False,
    )
```

```python
import math

import jax
import jax.numpy as jnp
from jax import lax
from jax.experimental import pallas as pl
from jax.experimental.pallas import tpu as pltpu
from jax.sharding import PartitionSpec as P

DIRS = 512
FREQS = 8
GRID = 1024
NODE_TILE = 256


def unit_phasor(turn):
    quarter = GRID // 4
    shifted = (turn + quarter // 2) & (GRID - 1)
    quadrant = shifted >> 8
    offset = (shifted & (quarter - 1)) - quarter // 2
    x = offset.astype(jnp.float32) * (2.0 * math.pi / GRID)
    x2 = x * x
    s = x * (1.0 + x2 * (-1.0 / 6 + x2 * (1.0 / 120 + x2 * (-1.0 / 5040 + x2 * (1.0 / 362880)))))
    c = 1.0 + x2 * (-0.5 + x2 * (1.0 / 24 + x2 * (-1.0 / 720 + x2 * (1.0 / 40320))))
    odd = (quadrant & 1) == 1
    cos_mag = jnp.where(odd, s, c)
    sin_mag = jnp.where(odd, c, s)
    cos_neg = (quadrant == 1) | (quadrant == 2)
    sin_neg = quadrant >= 2
    return jnp.where(cos_neg, -cos_mag, cos_mag), jnp.where(sin_neg, -sin_mag, sin_mag)


def amp_kernel(proj_ref, spread_ref, resp_ref, out_ref):
    @pl.when(pl.program_id(0) == 0)
    def _():
        out_ref[...] = jnp.zeros_like(out_ref)

    proj = proj_ref[...]
    base_c, base_s = unit_phasor(proj & (GRID - 1))
    rows = resp_ref.shape[2]
    cos_f, sin_f = base_c, base_s
    for f in range(FREQS):
        if f > 0:
            cos_f, sin_f = (
                cos_f * base_c - sin_f * base_s,
                sin_f * base_c + cos_f * base_s,
            )
        spread = spread_ref[f : f + 1, :]
        load_re = (spread * cos_f).astype(jnp.bfloat16)
        load_im = (-spread * sin_f).astype(jnp.bfloat16)
        resp = resp_ref[:, f].reshape(2 * rows, resp_ref.shape[3])
        by_re = jnp.dot(resp, load_re, preferred_element_type=jnp.float32)
        by_im = jnp.dot(resp, load_im, preferred_element_type=jnp.float32)
        out_ref[f, :, :DIRS] += by_re[:rows] - by_im[rows:]
        out_ref[f, :, DIRS:] += by_im[:rows] + by_re[rows:]


def partial_amplitudes(freq_resp, project, spread):
    nodes = project.shape[0]
    rows = freq_resp.shape[2]
    return pl.pallas_call(
        amp_kernel,
        out_shape=jax.ShapeDtypeStruct((FREQS, rows, 2 * DIRS), jnp.float32),
        grid=(nodes // NODE_TILE,),
        in_specs=[
            pl.BlockSpec((NODE_TILE, DIRS), lambda j: (j, 0)),
            pl.BlockSpec((FREQS, DIRS), lambda j: (0, 0)),
            pl.BlockSpec((2, FREQS, rows, NODE_TILE), lambda j: (0, 0, 0, j)),
        ],
        out_specs=pl.BlockSpec((FREQS, rows, 2 * DIRS), lambda j: (0, 0, 0)),
        compiler_params=pltpu.CompilerParams(dimension_semantics=("arbitrary",)),
    )(project, spread, freq_resp)


def gather_cols(amplitudes):
    freqs, piece, width = amplitudes.shape
    along_z = gather_by_permutes(amplitudes, "zlo", lax.axis_size("zlo"))
    along_z, amplitudes = lax.optimization_barrier((along_z, amplitudes))
    rows = gather_rows(amplitudes)
    mine = lax.all_gather(along_z, "drow", axis=0)
    mine, rows = lax.optimization_barrier((mine, rows))
    theirs = lax.ppermute(mine, "core", perm=[(0, 1), (1, 0)])
    return mine, theirs, rows


def spec_kernel(core_ref, rows_ref, mine_ref, theirs_ref, out_ref):
    rows = rows_ref[0]
    rows_im = jnp.concatenate([rows[:, DIRS:], -rows[:, :DIRS]], axis=1)
    first = core_ref[0] == 0
    contract = (((1,), (1,)), ((), ()))

    def dot(a, b):
        return lax.dot_general(a, b, contract, preferred_element_type=jnp.float32)

    zlo_count = mine_ref.shape[1]
    block = 2 * mine_ref.shape[0] * mine_ref.shape[3]
    for z in range(zlo_count):
        own = mine_ref[:, z, 0].reshape(-1, mine_ref.shape[-1])
        other = theirs_ref[:, z, 0].reshape(-1, mine_ref.shape[-1])
        cols = jnp.where(
            first, jnp.concatenate([own, other], axis=0), jnp.concatenate([other, own], axis=0)
        )
        out_ref[0, 0, :, z * block : (z + 1) * block] = dot(rows, cols)
        out_ref[1, 0, :, z * block : (z + 1) * block] = dot(rows_im, cols)


def cross_spectra(rows, mine, theirs):
    freqs, row_count, width = rows.shape
    col_count = 2 * mine.shape[0] * mine.shape[1] * mine.shape[3]
    core = lax.axis_index("core").astype(jnp.int32).reshape(1)
    col_spec = pl.BlockSpec(mine.shape[:2] + (1,) + mine.shape[3:], lambda f: (0, 0, f, 0, 0))
    return pl.pallas_call(
        spec_kernel,
        out_shape=jax.ShapeDtypeStruct((2, freqs, row_count, col_count), jnp.float32),
        grid=(freqs,),
        in_specs=[
            pl.BlockSpec(memory_space=pltpu.SMEM),
            pl.BlockSpec((1, row_count, width), lambda f: (f, 0, 0)),
            col_spec,
            col_spec,
        ],
        out_specs=pl.BlockSpec((2, 1, row_count, col_count), lambda f: (0, f, 0, 0)),
        compiler_params=pltpu.CompilerParams(dimension_semantics=("arbitrary",)),
    )(core, rows, mine, theirs)


def gather_by_permutes(piece, axis_name, count):
    ahead = [piece]
    for shift in range(1, count):
        ahead.append(
            lax.ppermute(piece, axis_name, perm=[(i, (i - shift) % count) for i in range(count)])
        )
    return jnp.roll(jnp.stack(ahead), lax.axis_index(axis_name), axis=0)


def gather_by_all_to_all(piece, axis_name, count):
    copies = jnp.broadcast_to(piece[None], (count,) + piece.shape)
    return lax.all_to_all(copies, axis_name, split_axis=0, concat_axis=0)


def gather_rows(amplitudes):
    count = lax.axis_size("zhi") * lax.axis_size("y")
    freqs, piece, width = amplitudes.shape
    pieces = gather_by_all_to_all(amplitudes, ("zhi", "y"), count)
    return pieces.transpose(1, 0, 2, 3).reshape(freqs, -1, width)


def reduce_over_nodes(partial_amp):
    freqs, dofs, width = partial_amp.shape
    zlo_count = lax.axis_size("zlo")
    split = partial_amp.reshape(freqs, zlo_count, 2, dofs // (2 * zlo_count), width)
    first = lax.axis_index("core") == 0
    keep = jnp.where(first, split[:, :, 0], split[:, :, 1])
    send = jnp.where(first, split[:, :, 1], split[:, :, 0])
    pair = keep + lax.ppermute(send, "core", perm=[(0, 1), (1, 0)])
    zlo = lax.axis_index("zlo")
    total = lax.dynamic_index_in_dim(pair, zlo, axis=1, keepdims=False)
    for shift in range(1, zlo_count):
        piece = lax.dynamic_index_in_dim(pair, (zlo + shift) % zlo_count, axis=1, keepdims=False)
        total = total + lax.ppermute(
            piece, "zlo", perm=[(i, (i + shift) % zlo_count) for i in range(zlo_count)]
        )
    return total


def local(freq_resp, node_coords, heading_steps, spectral_weights):
    project = (
        node_coords[0][:, None] * heading_steps[0][None, :]
        + node_coords[1][:, None] * heading_steps[1][None, :]
    )
    spread = jnp.sqrt(spectral_weights.astype(jnp.float32) / (64.0 * DIRS))
    partial_amp = partial_amplitudes(freq_resp, project, spread)
    amplitudes = reduce_over_nodes(partial_amp).astype(jnp.bfloat16)
    mine, theirs, rows = gather_cols(amplitudes)
    return cross_spectra(rows, mine, theirs)[:, :, None]


def solution(mesh):
    from jax.sharding import Mesh
    fine = Mesh(mesh.devices.reshape(4, 2, 4, 2, 4), ("zlo", "core", "drow", "zhi", "y"))
    placed = (P(None, None, ("drow", "zhi", "y"), ("zlo", "core")), P(None, ("zlo", "core")), P(), P())
    return jax.shard_map(
        local,
        mesh=fine,
        in_specs=placed,
        out_specs=P(None, None, "drow", ("zlo", "core"), ("zhi", "y")),
        check_vma=False,
    )
```

```python
import math

import jax
import jax.numpy as jnp
from jax import lax
from jax.experimental import pallas as pl
from jax.experimental.pallas import tpu as pltpu
from jax.sharding import PartitionSpec as P

DIRS = 512
FREQS = 8
GRID = 1024
NODE_TILE = 256


def unit_phasor(turn):
    quarter = GRID // 4
    shifted = (turn + quarter // 2) & (GRID - 1)
    quadrant = shifted >> 8
    offset = (shifted & (quarter - 1)) - quarter // 2
    x = offset.astype(jnp.float32) * (2.0 * math.pi / GRID)
    x2 = x * x
    s = x * (1.0 + x2 * (-1.0 / 6 + x2 * (1.0 / 120 + x2 * (-1.0 / 5040 + x2 * (1.0 / 362880)))))
    c = 1.0 + x2 * (-0.5 + x2 * (1.0 / 24 + x2 * (-1.0 / 720 + x2 * (1.0 / 40320))))
    odd = (quadrant & 1) == 1
    cos_mag = jnp.where(odd, s, c)
    sin_mag = jnp.where(odd, c, s)
    cos_neg = (quadrant == 1) | (quadrant == 2)
    sin_neg = quadrant >= 2
    return jnp.where(cos_neg, -cos_mag, cos_mag), jnp.where(sin_neg, -sin_mag, sin_mag)


def amp_kernel(proj_ref, spread_ref, resp_ref, out_ref):
    @pl.when(pl.program_id(0) == 0)
    def _():
        out_ref[...] = jnp.zeros_like(out_ref)

    proj = proj_ref[...]
    base_c, base_s = unit_phasor(proj & (GRID - 1))
    rows = resp_ref.shape[2]
    cos_f, sin_f = base_c, base_s
    for f in range(FREQS):
        if f > 0:
            cos_f, sin_f = (
                cos_f * base_c - sin_f * base_s,
                sin_f * base_c + cos_f * base_s,
            )
        spread = spread_ref[f : f + 1, :]
        load_re = (spread * cos_f).astype(jnp.bfloat16)
        load_im = (-spread * sin_f).astype(jnp.bfloat16)
        resp = resp_ref[:, f].reshape(2 * rows, resp_ref.shape[3])
        by_re = jnp.dot(resp, load_re, preferred_element_type=jnp.float32)
        by_im = jnp.dot(resp, load_im, preferred_element_type=jnp.float32)
        out_ref[f, :, :DIRS] += by_re[:rows] - by_im[rows:]
        out_ref[f, :, DIRS:] += by_im[:rows] + by_re[rows:]


def partial_amplitudes(freq_resp, project, spread):
    nodes = project.shape[0]
    rows = freq_resp.shape[2]
    return pl.pallas_call(
        amp_kernel,
        out_shape=jax.ShapeDtypeStruct((FREQS, rows, 2 * DIRS), jnp.float32),
        grid=(nodes // NODE_TILE,),
        in_specs=[
            pl.BlockSpec((NODE_TILE, DIRS), lambda j: (j, 0)),
            pl.BlockSpec((FREQS, DIRS), lambda j: (0, 0)),
            pl.BlockSpec((2, FREQS, rows, NODE_TILE), lambda j: (0, 0, 0, j)),
        ],
        out_specs=pl.BlockSpec((FREQS, rows, 2 * DIRS), lambda j: (0, 0, 0)),
        compiler_params=pltpu.CompilerParams(dimension_semantics=("arbitrary",)),
    )(project, spread, freq_resp)


def gather_cols(amplitudes):
    freqs, piece, width = amplitudes.shape
    along_z = gather_by_permutes(amplitudes, "zlo", lax.axis_size("zlo"))
    along_z, amplitudes = lax.optimization_barrier((along_z, amplitudes))
    rows = gather_rows(amplitudes)
    mine = lax.all_gather(along_z, "drow", axis=0)
    mine, rows = lax.optimization_barrier((mine, rows))
    theirs = lax.ppermute(mine, "core", perm=[(0, 1), (1, 0)])
    return mine, theirs, rows


def spec_kernel(core_ref, rows_ref, mine_ref, theirs_ref, out_ref):
    rows = rows_ref[0]
    rows_im = jnp.concatenate([rows[:, DIRS:], -rows[:, :DIRS]], axis=1)
    first = core_ref[0] == 0
    contract = (((1,), (1,)), ((), ()))

    def dot(a, b):
        return lax.dot_general(a, b, contract, preferred_element_type=jnp.float32)

    zlo_count = mine_ref.shape[1]
    block = 2 * mine_ref.shape[0] * mine_ref.shape[3]
    for z in range(zlo_count):
        own = mine_ref[:, z, 0].reshape(-1, mine_ref.shape[-1])
        other = theirs_ref[:, z, 0].reshape(-1, mine_ref.shape[-1])
        cols = jnp.where(
            first, jnp.concatenate([own, other], axis=0), jnp.concatenate([other, own], axis=0)
        )
        out_ref[0, 0, :, z * block : (z + 1) * block] = dot(rows, cols)
        out_ref[1, 0, :, z * block : (z + 1) * block] = dot(rows_im, cols)


def cross_spectra(rows, mine, theirs):
    freqs, row_count, width = rows.shape
    col_count = 2 * mine.shape[0] * mine.shape[1] * mine.shape[3]
    core = lax.axis_index("core").astype(jnp.int32).reshape(1)
    col_spec = pl.BlockSpec(mine.shape[:2] + (1,) + mine.shape[3:], lambda f: (0, 0, f, 0, 0))
    return pl.pallas_call(
        spec_kernel,
        out_shape=jax.ShapeDtypeStruct((2, freqs, row_count, col_count), jnp.float32),
        grid=(freqs,),
        in_specs=[
            pl.BlockSpec(memory_space=pltpu.SMEM),
            pl.BlockSpec((1, row_count, width), lambda f: (f, 0, 0)),
            col_spec,
            col_spec,
        ],
        out_specs=pl.BlockSpec((2, 1, row_count, col_count), lambda f: (0, f, 0, 0)),
        compiler_params=pltpu.CompilerParams(dimension_semantics=("arbitrary",)),
    )(core, rows, mine, theirs)


def gather_by_permutes(piece, axis_name, count):
    ahead = [piece]
    for shift in range(1, count):
        ahead.append(
            lax.ppermute(piece, axis_name, perm=[(i, (i - shift) % count) for i in range(count)])
        )
    return jnp.roll(jnp.stack(ahead), lax.axis_index(axis_name), axis=0)


def gather_by_all_to_all(piece, axis_name, count):
    copies = jnp.broadcast_to(piece[None], (count,) + piece.shape)
    return lax.all_to_all(copies, axis_name, split_axis=0, concat_axis=0)


def gather_rows(amplitudes):
    count = lax.axis_size("zhi") * lax.axis_size("y")
    freqs, piece, width = amplitudes.shape
    pieces = gather_by_permutes(amplitudes, ("zhi", "y"), count)
    return pieces.transpose(1, 0, 2, 3).reshape(freqs, -1, width)


def local(freq_resp, node_coords, heading_steps, spectral_weights):
    project = (
        node_coords[0][:, None] * heading_steps[0][None, :]
        + node_coords[1][:, None] * heading_steps[1][None, :]
    )
    spread = jnp.sqrt(spectral_weights.astype(jnp.float32) / (64.0 * DIRS))
    partial_amp = partial_amplitudes(freq_resp, project, spread)
    amplitudes = lax.psum_scatter(partial_amp, ("zlo", "core"), scatter_dimension=1, tiled=True).astype(
        jnp.bfloat16
    )
    mine, theirs, rows = gather_cols(amplitudes)
    return cross_spectra(rows, mine, theirs)[:, :, None]


def solution(mesh):
    from jax.sharding import Mesh
    fine = Mesh(mesh.devices.reshape(4, 2, 4, 2, 4), ("zlo", "core", "drow", "zhi", "y"))
    placed = (P(None, None, ("drow", "zhi", "y"), ("zlo", "core")), P(None, ("zlo", "core")), P(), P())
    return jax.shard_map(
        local,
        mesh=fine,
        in_specs=placed,
        out_specs=P(None, None, "drow", ("zlo", "core"), ("zhi", "y")),
        check_vma=False,
    )
```

```python
import math

import jax
import jax.numpy as jnp
from jax import lax
from jax.experimental import pallas as pl
from jax.experimental.pallas import tpu as pltpu
from jax.sharding import PartitionSpec as P

DIRS = 512
FREQS = 8
GRID = 1024
NODE_TILE = 256


def unit_phasor(turn):
    quarter = GRID // 4
    shifted = (turn + quarter // 2) & (GRID - 1)
    quadrant = shifted >> 8
    offset = (shifted & (quarter - 1)) - quarter // 2
    x = offset.astype(jnp.float32) * (2.0 * math.pi / GRID)
    x2 = x * x
    s = x * (1.0 + x2 * (-1.0 / 6 + x2 * (1.0 / 120 + x2 * (-1.0 / 5040 + x2 * (1.0 / 362880)))))
    c = 1.0 + x2 * (-0.5 + x2 * (1.0 / 24 + x2 * (-1.0 / 720 + x2 * (1.0 / 40320))))
    odd = (quadrant & 1) == 1
    cos_mag = jnp.where(odd, s, c)
    sin_mag = jnp.where(odd, c, s)
    cos_neg = (quadrant == 1) | (quadrant == 2)
    sin_neg = quadrant >= 2
    return jnp.where(cos_neg, -cos_mag, cos_mag), jnp.where(sin_neg, -sin_mag, sin_mag)


def amp_kernel(proj_ref, spread_ref, resp_ref, out_ref):
    @pl.when(pl.program_id(0) == 0)
    def _():
        out_ref[...] = jnp.zeros_like(out_ref)

    proj = proj_ref[...]
    base_c, base_s = unit_phasor(proj & (GRID - 1))
    rows = resp_ref.shape[2]
    cos_f, sin_f = base_c, base_s
    for f in range(FREQS):
        if f > 0:
            cos_f, sin_f = (
                cos_f * base_c - sin_f * base_s,
                sin_f * base_c + cos_f * base_s,
            )
        spread = spread_ref[f : f + 1, :]
        load_re = (spread * cos_f).astype(jnp.bfloat16)
        load_im = (-spread * sin_f).astype(jnp.bfloat16)
        resp = resp_ref[:, f].reshape(2 * rows, resp_ref.shape[3])
        by_re = jnp.dot(resp, load_re, preferred_element_type=jnp.float32)
        by_im = jnp.dot(resp, load_im, preferred_element_type=jnp.float32)
        out_ref[f, :, :DIRS] += by_re[:rows] - by_im[rows:]
        out_ref[f, :, DIRS:] += by_im[:rows] + by_re[rows:]


def partial_amplitudes(freq_resp, project, spread):
    nodes = project.shape[0]
    rows = freq_resp.shape[2]
    return pl.pallas_call(
        amp_kernel,
        out_shape=jax.ShapeDtypeStruct((FREQS, rows, 2 * DIRS), jnp.float32),
        grid=(nodes // NODE_TILE,),
        in_specs=[
            pl.BlockSpec((NODE_TILE, DIRS), lambda j: (j, 0)),
            pl.BlockSpec((FREQS, DIRS), lambda j: (0, 0)),
            pl.BlockSpec((2, FREQS, rows, NODE_TILE), lambda j: (0, 0, 0, j)),
        ],
        out_specs=pl.BlockSpec((FREQS, rows, 2 * DIRS), lambda j: (0, 0, 0)),
        compiler_params=pltpu.CompilerParams(dimension_semantics=("arbitrary",)),
    )(project, spread, freq_resp)


def gather_cols(amplitudes):
    freqs, piece, width = amplitudes.shape
    along_z = gather_by_permutes(amplitudes, "zlo", lax.axis_size("zlo"))
    same_half = gather_by_permutes(amplitudes, "y", lax.axis_size("y"))
    along_z, same_half, amplitudes = lax.optimization_barrier((along_z, same_half, amplitudes))
    other_half = from_other_half(amplitudes)
    mine = lax.all_gather(along_z, "drow", axis=0)
    mine, other_half = lax.optimization_barrier((mine, other_half))
    rows = join_rows(same_half, other_half)
    theirs = lax.ppermute(mine, "core", perm=[(0, 1), (1, 0)])
    return mine, theirs, rows


def spec_kernel(core_ref, rows_ref, mine_ref, theirs_ref, out_ref):
    rows = rows_ref[0]
    rows_im = jnp.concatenate([rows[:, DIRS:], -rows[:, :DIRS]], axis=1)
    first = core_ref[0] == 0
    contract = (((1,), (1,)), ((), ()))

    def dot(a, b):
        return lax.dot_general(a, b, contract, preferred_element_type=jnp.float32)

    zlo_count = mine_ref.shape[1]
    block = 2 * mine_ref.shape[0] * mine_ref.shape[3]
    for z in range(zlo_count):
        own = mine_ref[:, z, 0].reshape(-1, mine_ref.shape[-1])
        other = theirs_ref[:, z, 0].reshape(-1, mine_ref.shape[-1])
        cols = jnp.where(
            first, jnp.concatenate([own, other], axis=0), jnp.concatenate([other, own], axis=0)
        )
        out_ref[0, 0, :, z * block : (z + 1) * block] = dot(rows, cols)
        out_ref[1, 0, :, z * block : (z + 1) * block] = dot(rows_im, cols)


def cross_spectra(rows, mine, theirs):
    freqs, row_count, width = rows.shape
    col_count = 2 * mine.shape[0] * mine.shape[1] * mine.shape[3]
    core = lax.axis_index("core").astype(jnp.int32).reshape(1)
    col_spec = pl.BlockSpec(mine.shape[:2] + (1,) + mine.shape[3:], lambda f: (0, 0, f, 0, 0))
    return pl.pallas_call(
        spec_kernel,
        out_shape=jax.ShapeDtypeStruct((2, freqs, row_count, col_count), jnp.float32),
        grid=(freqs,),
        in_specs=[
            pl.BlockSpec(memory_space=pltpu.SMEM),
            pl.BlockSpec((1, row_count, width), lambda f: (f, 0, 0)),
            col_spec,
            col_spec,
        ],
        out_specs=pl.BlockSpec((2, 1, row_count, col_count), lambda f: (0, f, 0, 0)),
        compiler_params=pltpu.CompilerParams(dimension_semantics=("arbitrary",)),
    )(core, rows, mine, theirs)


def gather_by_permutes(piece, axis_name, count):
    ahead = [piece]
    for shift in range(1, count):
        ahead.append(
            lax.ppermute(piece, axis_name, perm=[(i, (i - shift) % count) for i in range(count)])
        )
    return jnp.roll(jnp.stack(ahead), lax.axis_index(axis_name), axis=0)


def gather_by_all_to_all(piece, axis_name, count):
    copies = jnp.broadcast_to(piece[None], (count,) + piece.shape)
    return lax.all_to_all(copies, axis_name, split_axis=0, concat_axis=0)


def from_other_half(piece):
    ys = lax.axis_size("y")
    flat = [(z, y) for z in range(lax.axis_size("zhi")) for y in range(ys)]
    ahead = []
    for shift in range(ys):
        perm = [(z * ys + y, (1 - z) * ys + (y - shift) % ys) for z, y in flat]
        ahead.append(lax.ppermute(piece, ("zhi", "y"), perm=perm))
    return jnp.roll(jnp.stack(ahead), lax.axis_index("y"), axis=0)


def join_rows(same_half, other_half):
    first = lax.axis_index("zhi") == 0
    halves = jnp.where(first, jnp.stack([same_half, other_half]), jnp.stack([other_half, same_half]))
    freqs, piece, width = halves.shape[2:]
    halves = halves.reshape(-1, freqs, piece, width)
    return halves.transpose(1, 0, 2, 3).reshape(freqs, -1, width)


def local(freq_resp, node_coords, heading_steps, spectral_weights):
    project = (
        node_coords[0][:, None] * heading_steps[0][None, :]
        + node_coords[1][:, None] * heading_steps[1][None, :]
    )
    spread = jnp.sqrt(spectral_weights.astype(jnp.float32) / (64.0 * DIRS))
    partial_amp = partial_amplitudes(freq_resp, project, spread)
    amplitudes = lax.psum_scatter(partial_amp, ("zlo", "core"), scatter_dimension=1, tiled=True).astype(
        jnp.bfloat16
    )
    mine, theirs, rows = gather_cols(amplitudes)
    return cross_spectra(rows, mine, theirs)[:, :, None]


def solution(mesh):
    from jax.sharding import Mesh
    fine = Mesh(mesh.devices.reshape(4, 2, 4, 2, 4), ("zlo", "core", "drow", "zhi", "y"))
    placed = (P(None, None, ("drow", "zhi", "y"), ("zlo", "core")), P(None, ("zlo", "core")), P(), P())
    return jax.shard_map(
        local,
        mesh=fine,
        in_specs=placed,
        out_specs=P(None, None, "drow", ("zlo", "core"), ("zhi", "y")),
        check_vma=False,
    )
```

```python
import math

import jax
import jax.numpy as jnp
from jax import lax
from jax.experimental import pallas as pl
from jax.experimental.pallas import tpu as pltpu
from jax.sharding import PartitionSpec as P

DIRS = 512
FREQS = 8
GRID = 1024
NODE_TILE = 256


def unit_phasor(turn):
    quarter = GRID // 4
    shifted = (turn + quarter // 2) & (GRID - 1)
    quadrant = shifted >> 8
    offset = (shifted & (quarter - 1)) - quarter // 2
    x = offset.astype(jnp.float32) * (2.0 * math.pi / GRID)
    x2 = x * x
    s = x * (1.0 + x2 * (-1.0 / 6 + x2 * (1.0 / 120 + x2 * (-1.0 / 5040 + x2 * (1.0 / 362880)))))
    c = 1.0 + x2 * (-0.5 + x2 * (1.0 / 24 + x2 * (-1.0 / 720 + x2 * (1.0 / 40320))))
    odd = (quadrant & 1) == 1
    cos_mag = jnp.where(odd, s, c)
    sin_mag = jnp.where(odd, c, s)
    cos_neg = (quadrant == 1) | (quadrant == 2)
    sin_neg = quadrant >= 2
    return jnp.where(cos_neg, -cos_mag, cos_mag), jnp.where(sin_neg, -sin_mag, sin_mag)


def amp_kernel(proj_ref, spread_ref, resp_ref, out_ref):
    @pl.when(pl.program_id(0) == 0)
    def _():
        out_ref[...] = jnp.zeros_like(out_ref)

    proj = proj_ref[...]
    base_c, base_s = unit_phasor(proj & (GRID - 1))
    rows = resp_ref.shape[2]
    cos_f, sin_f = base_c, base_s
    for f in range(FREQS):
        if f > 0:
            cos_f, sin_f = (
                cos_f * base_c - sin_f * base_s,
                sin_f * base_c + cos_f * base_s,
            )
        spread = spread_ref[f : f + 1, :]
        load_re = (spread * cos_f).astype(jnp.bfloat16)
        load_im = (-spread * sin_f).astype(jnp.bfloat16)
        resp = resp_ref[:, f].reshape(2 * rows, resp_ref.shape[3])
        by_re = jnp.dot(resp, load_re, preferred_element_type=jnp.float32)
        by_im = jnp.dot(resp, load_im, preferred_element_type=jnp.float32)
        out_ref[f, :, :DIRS] += by_re[:rows] - by_im[rows:]
        out_ref[f, :, DIRS:] += by_im[:rows] + by_re[rows:]


def partial_amplitudes(freq_resp, project, spread):
    nodes = project.shape[0]
    rows = freq_resp.shape[2]
    return pl.pallas_call(
        amp_kernel,
        out_shape=jax.ShapeDtypeStruct((FREQS, rows, 2 * DIRS), jnp.float32),
        grid=(nodes // NODE_TILE,),
        in_specs=[
            pl.BlockSpec((NODE_TILE, DIRS), lambda j: (j, 0)),
            pl.BlockSpec((FREQS, DIRS), lambda j: (0, 0)),
            pl.BlockSpec((2, FREQS, rows, NODE_TILE), lambda j: (0, 0, 0, j)),
        ],
        out_specs=pl.BlockSpec((FREQS, rows, 2 * DIRS), lambda j: (0, 0, 0)),
        compiler_params=pltpu.CompilerParams(dimension_semantics=("arbitrary",)),
    )(project, spread, freq_resp)


def gather_cols(amplitudes):
    freqs, piece, width = amplitudes.shape
    along_z = gather_by_permutes(amplitudes, "zlo", lax.axis_size("zlo"))
    same_half = gather_by_permutes(amplitudes, "y", lax.axis_size("y"))
    along_z, same_half, amplitudes = lax.optimization_barrier((along_z, same_half, amplitudes))
    other_half = from_other_half(amplitudes)
    half = along_z.shape[1] // 2
    mine = jnp.concatenate(
        [
            lax.all_gather(along_z[:, :half], "drow", axis=0),
            gather_by_permutes(along_z[:, half:], "drow", lax.axis_size("drow")),
        ],
        axis=2,
    )
    mine, other_half = lax.optimization_barrier((mine, other_half))
    rows = join_rows(same_half, other_half)
    theirs = lax.ppermute(mine, "core", perm=[(0, 1), (1, 0)])
    return mine, theirs, rows


def spec_kernel(core_ref, rows_ref, mine_ref, theirs_ref, out_ref):
    rows = rows_ref[0]
    rows_im = jnp.concatenate([rows[:, DIRS:], -rows[:, :DIRS]], axis=1)
    first = core_ref[0] == 0
    contract = (((1,), (1,)), ((), ()))

    def dot(a, b):
        return lax.dot_general(a, b, contract, preferred_element_type=jnp.float32)

    zlo_count = mine_ref.shape[1]
    block = 2 * mine_ref.shape[0] * mine_ref.shape[3]
    for z in range(zlo_count):
        own = mine_ref[:, z, 0].reshape(-1, mine_ref.shape[-1])
        other = theirs_ref[:, z, 0].reshape(-1, mine_ref.shape[-1])
        cols = jnp.where(
            first, jnp.concatenate([own, other], axis=0), jnp.concatenate([other, own], axis=0)
        )
        out_ref[0, 0, :, z * block : (z + 1) * block] = dot(rows, cols)
        out_ref[1, 0, :, z * block : (z + 1) * block] = dot(rows_im, cols)


def cross_spectra(rows, mine, theirs):
    freqs, row_count, width = rows.shape
    col_count = 2 * mine.shape[0] * mine.shape[1] * mine.shape[3]
    core = lax.axis_index("core").astype(jnp.int32).reshape(1)
    col_spec = pl.BlockSpec(mine.shape[:2] + (1,) + mine.shape[3:], lambda f: (0, 0, f, 0, 0))
    return pl.pallas_call(
        spec_kernel,
        out_shape=jax.ShapeDtypeStruct((2, freqs, row_count, col_count), jnp.float32),
        grid=(freqs,),
        in_specs=[
            pl.BlockSpec(memory_space=pltpu.SMEM),
            pl.BlockSpec((1, row_count, width), lambda f: (f, 0, 0)),
            col_spec,
            col_spec,
        ],
        out_specs=pl.BlockSpec((2, 1, row_count, col_count), lambda f: (0, f, 0, 0)),
        compiler_params=pltpu.CompilerParams(dimension_semantics=("arbitrary",)),
    )(core, rows, mine, theirs)


def gather_by_permutes(piece, axis_name, count):
    ahead = [piece]
    for shift in range(1, count):
        ahead.append(
            lax.ppermute(piece, axis_name, perm=[(i, (i - shift) % count) for i in range(count)])
        )
    return jnp.roll(jnp.stack(ahead), lax.axis_index(axis_name), axis=0)


def gather_by_all_to_all(piece, axis_name, count):
    copies = jnp.broadcast_to(piece[None], (count,) + piece.shape)
    return lax.all_to_all(copies, axis_name, split_axis=0, concat_axis=0)


def from_other_half(piece):
    ys = lax.axis_size("y")
    flat = [(z, y) for z in range(lax.axis_size("zhi")) for y in range(ys)]
    ahead = []
    for shift in range(ys):
        perm = [(z * ys + y, (1 - z) * ys + (y - shift) % ys) for z, y in flat]
        ahead.append(lax.ppermute(piece, ("zhi", "y"), perm=perm))
    return jnp.roll(jnp.stack(ahead), lax.axis_index("y"), axis=0)


def join_rows(same_half, other_half):
    first = lax.axis_index("zhi") == 0
    halves = jnp.where(first, jnp.stack([same_half, other_half]), jnp.stack([other_half, same_half]))
    freqs, piece, width = halves.shape[2:]
    halves = halves.reshape(-1, freqs, piece, width)
    return halves.transpose(1, 0, 2, 3).reshape(freqs, -1, width)


def local(freq_resp, node_coords, heading_steps, spectral_weights):
    project = (
        node_coords[0][:, None] * heading_steps[0][None, :]
        + node_coords[1][:, None] * heading_steps[1][None, :]
    )
    spread = jnp.sqrt(spectral_weights.astype(jnp.float32) / (64.0 * DIRS))
    partial_amp = partial_amplitudes(freq_resp, project, spread)
    amplitudes = lax.psum_scatter(partial_amp, ("zlo", "core"), scatter_dimension=1, tiled=True).astype(
        jnp.bfloat16
    )
    mine, theirs, rows = gather_cols(amplitudes)
    return cross_spectra(rows, mine, theirs)[:, :, None]


def solution(mesh):
    from jax.sharding import Mesh
    fine = Mesh(mesh.devices.reshape(4, 2, 4, 2, 4), ("zlo", "core", "drow", "zhi", "y"))
    placed = (P(None, None, ("drow", "zhi", "y"), ("zlo", "core")), P(None, ("zlo", "core")), P(), P())
    return jax.shard_map(
        local,
        mesh=fine,
        in_specs=placed,
        out_specs=P(None, None, "drow", ("zlo", "core"), ("zhi", "y")),
        check_vma=False,
    )
```

```python
import math

import jax
import jax.numpy as jnp
from jax import lax
from jax.experimental import pallas as pl
from jax.experimental.pallas import tpu as pltpu
from jax.sharding import PartitionSpec as P

DIRS = 512
FREQS = 8
GRID = 1024
NODE_TILE = 512


def unit_phasor(turn):
    quarter = GRID // 4
    shifted = (turn + quarter // 2) & (GRID - 1)
    quadrant = shifted >> 8
    offset = (shifted & (quarter - 1)) - quarter // 2
    x = offset.astype(jnp.float32) * (2.0 * math.pi / GRID)
    x2 = x * x
    s = x * (1.0 + x2 * (-1.0 / 6 + x2 * (1.0 / 120 + x2 * (-1.0 / 5040 + x2 * (1.0 / 362880)))))
    c = 1.0 + x2 * (-0.5 + x2 * (1.0 / 24 + x2 * (-1.0 / 720 + x2 * (1.0 / 40320))))
    odd = (quadrant & 1) == 1
    cos_mag = jnp.where(odd, s, c)
    sin_mag = jnp.where(odd, c, s)
    cos_neg = (quadrant == 1) | (quadrant == 2)
    sin_neg = quadrant >= 2
    return jnp.where(cos_neg, -cos_mag, cos_mag), jnp.where(sin_neg, -sin_mag, sin_mag)


def amp_kernel(proj_ref, spread_ref, resp_ref, out_ref):
    @pl.when(pl.program_id(0) == 0)
    def _():
        out_ref[...] = jnp.zeros_like(out_ref)

    proj = proj_ref[...]
    base_c, base_s = unit_phasor(proj & (GRID - 1))
    rows = resp_ref.shape[2]
    cos_f, sin_f = base_c, base_s
    for f in range(FREQS):
        if f > 0:
            cos_f, sin_f = (
                cos_f * base_c - sin_f * base_s,
                sin_f * base_c + cos_f * base_s,
            )
        spread = spread_ref[f : f + 1, :]
        load_re = (spread * cos_f).astype(jnp.bfloat16)
        load_im = (-spread * sin_f).astype(jnp.bfloat16)
        resp = resp_ref[:, f].reshape(2 * rows, resp_ref.shape[3])
        by_re = jnp.dot(resp, load_re, preferred_element_type=jnp.float32)
        by_im = jnp.dot(resp, load_im, preferred_element_type=jnp.float32)
        out_ref[f, :, :DIRS] += by_re[:rows] - by_im[rows:]
        out_ref[f, :, DIRS:] += by_im[:rows] + by_re[rows:]


def partial_amplitudes(freq_resp, project, spread):
    nodes = project.shape[0]
    rows = freq_resp.shape[2]
    return pl.pallas_call(
        amp_kernel,
        out_shape=jax.ShapeDtypeStruct((FREQS, rows, 2 * DIRS), jnp.float32),
        grid=(nodes // NODE_TILE,),
        in_specs=[
            pl.BlockSpec((NODE_TILE, DIRS), lambda j: (j, 0)),
            pl.BlockSpec((FREQS, DIRS), lambda j: (0, 0)),
            pl.BlockSpec((2, FREQS, rows, NODE_TILE), lambda j: (0, 0, 0, j)),
        ],
        out_specs=pl.BlockSpec((FREQS, rows, 2 * DIRS), lambda j: (0, 0, 0)),
        compiler_params=pltpu.CompilerParams(dimension_semantics=("arbitrary",)),
    )(project, spread, freq_resp)


def gather_cols(amplitudes):
    freqs, piece, width = amplitudes.shape
    along_z = gather_by_permutes(amplitudes, "zlo", lax.axis_size("zlo"))
    same_half = gather_by_permutes(amplitudes, "y", lax.axis_size("y"))
    along_z, same_half, amplitudes = lax.optimization_barrier((along_z, same_half, amplitudes))
    other_half = from_other_half(amplitudes)
    mine = lax.all_gather(along_z, "drow", axis=0)
    mine, other_half = lax.optimization_barrier((mine, other_half))
    rows = join_rows(same_half, other_half)
    theirs = lax.ppermute(mine, "core", perm=[(0, 1), (1, 0)])
    return mine, theirs, rows


def spec_kernel(core_ref, rows_ref, mine_ref, theirs_ref, out_ref):
    rows = rows_ref[0]
    rows_im = jnp.concatenate([rows[:, DIRS:], -rows[:, :DIRS]], axis=1)
    first = core_ref[0] == 0
    contract = (((1,), (1,)), ((), ()))

    def dot(a, b):
        return lax.dot_general(a, b, contract, preferred_element_type=jnp.float32)

    zlo_count = mine_ref.shape[1]
    block = 2 * mine_ref.shape[0] * mine_ref.shape[3]
    for z in range(zlo_count):
        own = mine_ref[:, z, 0].reshape(-1, mine_ref.shape[-1])
        other = theirs_ref[:, z, 0].reshape(-1, mine_ref.shape[-1])
        cols = jnp.where(
            first, jnp.concatenate([own, other], axis=0), jnp.concatenate([other, own], axis=0)
        )
        out_ref[0, 0, :, z * block : (z + 1) * block] = dot(rows, cols)
        out_ref[1, 0, :, z * block : (z + 1) * block] = dot(rows_im, cols)


def cross_spectra(rows, mine, theirs):
    freqs, row_count, width = rows.shape
    col_count = 2 * mine.shape[0] * mine.shape[1] * mine.shape[3]
    core = lax.axis_index("core").astype(jnp.int32).reshape(1)
    col_spec = pl.BlockSpec(mine.shape[:2] + (1,) + mine.shape[3:], lambda f: (0, 0, f, 0, 0))
    return pl.pallas_call(
        spec_kernel,
        out_shape=jax.ShapeDtypeStruct((2, freqs, row_count, col_count), jnp.float32),
        grid=(freqs,),
        in_specs=[
            pl.BlockSpec(memory_space=pltpu.SMEM),
            pl.BlockSpec((1, row_count, width), lambda f: (f, 0, 0)),
            col_spec,
            col_spec,
        ],
        out_specs=pl.BlockSpec((2, 1, row_count, col_count), lambda f: (0, f, 0, 0)),
        compiler_params=pltpu.CompilerParams(dimension_semantics=("arbitrary",)),
    )(core, rows, mine, theirs)


def gather_by_permutes(piece, axis_name, count):
    ahead = [piece]
    for shift in range(1, count):
        ahead.append(
            lax.ppermute(piece, axis_name, perm=[(i, (i - shift) % count) for i in range(count)])
        )
    return jnp.roll(jnp.stack(ahead), lax.axis_index(axis_name), axis=0)


def gather_by_all_to_all(piece, axis_name, count):
    copies = jnp.broadcast_to(piece[None], (count,) + piece.shape)
    return lax.all_to_all(copies, axis_name, split_axis=0, concat_axis=0)


def from_other_half(piece):
    ys = lax.axis_size("y")
    flat = [(z, y) for z in range(lax.axis_size("zhi")) for y in range(ys)]
    ahead = []
    for shift in range(ys):
        perm = [(z * ys + y, (1 - z) * ys + (y - shift) % ys) for z, y in flat]
        ahead.append(lax.ppermute(piece, ("zhi", "y"), perm=perm))
    return jnp.roll(jnp.stack(ahead), lax.axis_index("y"), axis=0)


def join_rows(same_half, other_half):
    first = lax.axis_index("zhi") == 0
    halves = jnp.where(first, jnp.stack([same_half, other_half]), jnp.stack([other_half, same_half]))
    freqs, piece, width = halves.shape[2:]
    halves = halves.reshape(-1, freqs, piece, width)
    return halves.transpose(1, 0, 2, 3).reshape(freqs, -1, width)


def local(freq_resp, node_coords, heading_steps, spectral_weights):
    project = (
        node_coords[0][:, None] * heading_steps[0][None, :]
        + node_coords[1][:, None] * heading_steps[1][None, :]
    )
    spread = jnp.sqrt(spectral_weights.astype(jnp.float32) / (64.0 * DIRS))
    partial_amp = partial_amplitudes(freq_resp, project, spread)
    amplitudes = lax.psum_scatter(partial_amp, ("zlo", "core"), scatter_dimension=1, tiled=True).astype(
        jnp.bfloat16
    )
    mine, theirs, rows = gather_cols(amplitudes)
    return cross_spectra(rows, mine, theirs)[:, :, None]


def solution(mesh):
    from jax.sharding import Mesh
    fine = Mesh(mesh.devices.reshape(4, 2, 4, 2, 4), ("zlo", "core", "drow", "zhi", "y"))
    placed = (P(None, None, ("drow", "zhi", "y"), ("zlo", "core")), P(None, ("zlo", "core")), P(), P())
    return jax.shard_map(
        local,
        mesh=fine,
        in_specs=placed,
        out_specs=P(None, None, "drow", ("zlo", "core"), ("zhi", "y")),
        check_vma=False,
    )
```

```python
import math

import jax
import jax.numpy as jnp
from jax import lax
from jax.experimental import pallas as pl
from jax.experimental.pallas import tpu as pltpu
from jax.sharding import PartitionSpec as P

DIRS = 512
FREQS = 8
GRID = 1024
NODE_TILE = 512


def unit_phasor(turn):
    quarter = GRID // 4
    shifted = (turn + quarter // 2) & (GRID - 1)
    quadrant = shifted >> 8
    offset = (shifted & (quarter - 1)) - quarter // 2
    x = offset.astype(jnp.float32) * (2.0 * math.pi / GRID)
    x2 = x * x
    s = x * (1.0 + x2 * (-1.0 / 6 + x2 * (1.0 / 120 + x2 * (-1.0 / 5040 + x2 * (1.0 / 362880)))))
    c = 1.0 + x2 * (-0.5 + x2 * (1.0 / 24 + x2 * (-1.0 / 720 + x2 * (1.0 / 40320))))
    odd = (quadrant & 1) == 1
    cos_mag = jnp.where(odd, s, c)
    sin_mag = jnp.where(odd, c, s)
    cos_neg = (quadrant == 1) | (quadrant == 2)
    sin_neg = quadrant >= 2
    return jnp.where(cos_neg, -cos_mag, cos_mag), jnp.where(sin_neg, -sin_mag, sin_mag)


def amp_kernel(proj_ref, spread_ref, resp_ref, out_ref):
    @pl.when(pl.program_id(0) == 0)
    def _():
        out_ref[...] = jnp.zeros_like(out_ref)

    proj = proj_ref[...]
    base_c, base_s = unit_phasor(proj & (GRID - 1))
    rows = resp_ref.shape[2]
    cos_f, sin_f = base_c, base_s
    for f in range(FREQS):
        if f > 0:
            cos_f, sin_f = (
                cos_f * base_c - sin_f * base_s,
                sin_f * base_c + cos_f * base_s,
            )
        spread = spread_ref[f : f + 1, :]
        load_re = (spread * cos_f).astype(jnp.bfloat16)
        load_im = (-spread * sin_f).astype(jnp.bfloat16)
        resp = resp_ref[:, f].reshape(2 * rows, resp_ref.shape[3])
        by_re = jnp.dot(resp, load_re, preferred_element_type=jnp.float32)
        by_im = jnp.dot(resp, load_im, preferred_element_type=jnp.float32)
        out_ref[f, :, :DIRS] += by_re[:rows] - by_im[rows:]
        out_ref[f, :, DIRS:] += by_im[:rows] + by_re[rows:]


def partial_amplitudes(freq_resp, project, spread):
    nodes = project.shape[0]
    rows = freq_resp.shape[2]
    return pl.pallas_call(
        amp_kernel,
        out_shape=jax.ShapeDtypeStruct((FREQS, rows, 2 * DIRS), jnp.float32),
        grid=(nodes // NODE_TILE,),
        in_specs=[
            pl.BlockSpec((NODE_TILE, DIRS), lambda j: (j, 0)),
            pl.BlockSpec((FREQS, DIRS), lambda j: (0, 0)),
            pl.BlockSpec((2, FREQS, rows, NODE_TILE), lambda j: (0, 0, 0, j)),
        ],
        out_specs=pl.BlockSpec((FREQS, rows, 2 * DIRS), lambda j: (0, 0, 0)),
        compiler_params=pltpu.CompilerParams(dimension_semantics=("arbitrary",)),
    )(project, spread, freq_resp)


def gather_cols(amplitudes):
    freqs, piece, width = amplitudes.shape
    along_z = gather_by_permutes(amplitudes, "zlo", lax.axis_size("zlo"))
    same_half = gather_by_permutes(amplitudes, "y", lax.axis_size("y"))
    along_z, same_half, amplitudes = lax.optimization_barrier((along_z, same_half, amplitudes))
    other_half = from_other_half(amplitudes)
    mine = lax.all_gather(along_z, "drow", axis=0)
    mine, other_half = lax.optimization_barrier((mine, other_half))
    rows = join_rows(same_half, other_half)
    theirs = lax.ppermute(mine, "core", perm=[(0, 1), (1, 0)])
    return mine, theirs, rows


def spec_kernel(core_ref, rows_ref, mine_ref, theirs_ref, out_ref):
    rows = rows_ref[0]
    rows_im = jnp.concatenate([rows[:, DIRS:], -rows[:, :DIRS]], axis=1)
    first = core_ref[0] == 0
    contract = (((1,), (1,)), ((), ()))

    def dot(a, b):
        return lax.dot_general(a, b, contract, preferred_element_type=jnp.float32)

    zlo_count = mine_ref.shape[1]
    block = 2 * mine_ref.shape[0] * mine_ref.shape[3]
    half = block // 2
    for z in range(zlo_count):
        own = mine_ref[:, z, 0].reshape(-1, mine_ref.shape[-1])
        other = theirs_ref[:, z, 0].reshape(-1, mine_ref.shape[-1])
        parts = (dot(rows, own), dot(rows_im, own), dot(rows, other), dot(rows_im, other))
        start = z * block

        @pl.when(first)
        def _():
            out_ref[0, 0, :, start : start + half] = parts[0]
            out_ref[1, 0, :, start : start + half] = parts[1]
            out_ref[0, 0, :, start + half : start + block] = parts[2]
            out_ref[1, 0, :, start + half : start + block] = parts[3]

        @pl.when(jnp.logical_not(first))
        def _():
            out_ref[0, 0, :, start : start + half] = parts[2]
            out_ref[1, 0, :, start : start + half] = parts[3]
            out_ref[0, 0, :, start + half : start + block] = parts[0]
            out_ref[1, 0, :, start + half : start + block] = parts[1]


def cross_spectra(rows, mine, theirs):
    freqs, row_count, width = rows.shape
    col_count = 2 * mine.shape[0] * mine.shape[1] * mine.shape[3]
    core = lax.axis_index("core").astype(jnp.int32).reshape(1)
    col_spec = pl.BlockSpec(mine.shape[:2] + (1,) + mine.shape[3:], lambda f: (0, 0, f, 0, 0))
    return pl.pallas_call(
        spec_kernel,
        out_shape=jax.ShapeDtypeStruct((2, freqs, row_count, col_count), jnp.float32),
        grid=(freqs,),
        in_specs=[
            pl.BlockSpec(memory_space=pltpu.SMEM),
            pl.BlockSpec((1, row_count, width), lambda f: (f, 0, 0)),
            col_spec,
            col_spec,
        ],
        out_specs=pl.BlockSpec((2, 1, row_count, col_count), lambda f: (0, f, 0, 0)),
        compiler_params=pltpu.CompilerParams(dimension_semantics=("arbitrary",)),
    )(core, rows, mine, theirs)


def gather_by_permutes(piece, axis_name, count):
    ahead = [piece]
    for shift in range(1, count):
        ahead.append(
            lax.ppermute(piece, axis_name, perm=[(i, (i - shift) % count) for i in range(count)])
        )
    return jnp.roll(jnp.stack(ahead), lax.axis_index(axis_name), axis=0)


def gather_by_all_to_all(piece, axis_name, count):
    copies = jnp.broadcast_to(piece[None], (count,) + piece.shape)
    return lax.all_to_all(copies, axis_name, split_axis=0, concat_axis=0)


def from_other_half(piece):
    ys = lax.axis_size("y")
    flat = [(z, y) for z in range(lax.axis_size("zhi")) for y in range(ys)]
    ahead = []
    for shift in range(ys):
        perm = [(z * ys + y, (1 - z) * ys + (y - shift) % ys) for z, y in flat]
        ahead.append(lax.ppermute(piece, ("zhi", "y"), perm=perm))
    return jnp.roll(jnp.stack(ahead), lax.axis_index("y"), axis=0)


def join_rows(same_half, other_half):
    first = lax.axis_index("zhi") == 0
    halves = jnp.where(first, jnp.stack([same_half, other_half]), jnp.stack([other_half, same_half]))
    freqs, piece, width = halves.shape[2:]
    halves = halves.reshape(-1, freqs, piece, width)
    return halves.transpose(1, 0, 2, 3).reshape(freqs, -1, width)


def local(freq_resp, node_coords, heading_steps, spectral_weights):
    project = (
        node_coords[0][:, None] * heading_steps[0][None, :]
        + node_coords[1][:, None] * heading_steps[1][None, :]
    )
    spread = jnp.sqrt(spectral_weights.astype(jnp.float32) / (64.0 * DIRS))
    partial_amp = partial_amplitudes(freq_resp, project, spread)
    amplitudes = lax.psum_scatter(partial_amp, ("zlo", "core"), scatter_dimension=1, tiled=True).astype(
        jnp.bfloat16
    )
    mine, theirs, rows = gather_cols(amplitudes)
    return cross_spectra(rows, mine, theirs)[:, :, None]


def solution(mesh):
    from jax.sharding import Mesh
    fine = Mesh(mesh.devices.reshape(4, 2, 4, 2, 4), ("zlo", "core", "drow", "zhi", "y"))
    placed = (P(None, None, ("drow", "zhi", "y"), ("zlo", "core")), P(None, ("zlo", "core")), P(), P())
    return jax.shard_map(
        local,
        mesh=fine,
        in_specs=placed,
        out_specs=P(None, None, "drow", ("zlo", "core"), ("zhi", "y")),
        check_vma=False,
    )
```

```python
import math

import jax
import jax.numpy as jnp
from jax import lax
from jax.experimental import pallas as pl
from jax.experimental.pallas import tpu as pltpu
from jax.sharding import PartitionSpec as P

DIRS = 512
FREQS = 8
GRID = 1024
NODE_TILE = 512
FREQ_BLOCK = 2


def unit_phasor(turn):
    quarter = GRID // 4
    shifted = (turn + quarter // 2) & (GRID - 1)
    quadrant = shifted >> 8
    offset = (shifted & (quarter - 1)) - quarter // 2
    x = offset.astype(jnp.float32) * (2.0 * math.pi / GRID)
    x2 = x * x
    s = x * (1.0 + x2 * (-1.0 / 6 + x2 * (1.0 / 120 + x2 * (-1.0 / 5040 + x2 * (1.0 / 362880)))))
    c = 1.0 + x2 * (-0.5 + x2 * (1.0 / 24 + x2 * (-1.0 / 720 + x2 * (1.0 / 40320))))
    odd = (quadrant & 1) == 1
    cos_mag = jnp.where(odd, s, c)
    sin_mag = jnp.where(odd, c, s)
    cos_neg = (quadrant == 1) | (quadrant == 2)
    sin_neg = quadrant >= 2
    return jnp.where(cos_neg, -cos_mag, cos_mag), jnp.where(sin_neg, -sin_mag, sin_mag)


def amp_kernel(proj_ref, spread_ref, resp_ref, out_ref):
    @pl.when(pl.program_id(0) == 0)
    def _():
        out_ref[...] = jnp.zeros_like(out_ref)

    proj = proj_ref[...]
    base_c, base_s = unit_phasor(proj & (GRID - 1))
    rows = resp_ref.shape[2]
    cos_f, sin_f = base_c, base_s
    for f in range(FREQS):
        if f > 0:
            cos_f, sin_f = (
                cos_f * base_c - sin_f * base_s,
                sin_f * base_c + cos_f * base_s,
            )
        spread = spread_ref[f : f + 1, :]
        load_re = (spread * cos_f).astype(jnp.bfloat16)
        load_im = (-spread * sin_f).astype(jnp.bfloat16)
        resp = resp_ref[:, f].reshape(2 * rows, resp_ref.shape[3])
        by_re = jnp.dot(resp, load_re, preferred_element_type=jnp.float32)
        by_im = jnp.dot(resp, load_im, preferred_element_type=jnp.float32)
        out_ref[f, :, :DIRS] += by_re[:rows] - by_im[rows:]
        out_ref[f, :, DIRS:] += by_im[:rows] + by_re[rows:]


def partial_amplitudes(freq_resp, project, spread):
    nodes = project.shape[0]
    rows = freq_resp.shape[2]
    return pl.pallas_call(
        amp_kernel,
        out_shape=jax.ShapeDtypeStruct((FREQS, rows, 2 * DIRS), jnp.float32),
        grid=(nodes // NODE_TILE,),
        in_specs=[
            pl.BlockSpec((NODE_TILE, DIRS), lambda j: (j, 0)),
            pl.BlockSpec((FREQS, DIRS), lambda j: (0, 0)),
            pl.BlockSpec((2, FREQS, rows, NODE_TILE), lambda j: (0, 0, 0, j)),
        ],
        out_specs=pl.BlockSpec((FREQS, rows, 2 * DIRS), lambda j: (0, 0, 0)),
        compiler_params=pltpu.CompilerParams(dimension_semantics=("arbitrary",)),
    )(project, spread, freq_resp)


def gather_cols(amplitudes):
    freqs, piece, width = amplitudes.shape
    along_z = gather_by_permutes(amplitudes, "zlo", lax.axis_size("zlo"))
    same_half = gather_by_permutes(amplitudes, "y", lax.axis_size("y"))
    along_z, same_half, amplitudes = lax.optimization_barrier((along_z, same_half, amplitudes))
    other_half = from_other_half(amplitudes)
    mine = lax.all_gather(along_z, "drow", axis=0)
    mine, other_half = lax.optimization_barrier((mine, other_half))
    rows = join_rows(same_half, other_half)
    theirs = lax.ppermute(mine, "core", perm=[(0, 1), (1, 0)])
    return mine, theirs, rows


def spec_kernel(core_ref, rows_ref, mine_ref, theirs_ref, out_ref):
    first = core_ref[0] == 0
    contract = (((1,), (1,)), ((), ()))

    def dot(a, b):
        return lax.dot_general(a, b, contract, preferred_element_type=jnp.float32)

    zlo_count = mine_ref.shape[1]
    block = 2 * mine_ref.shape[0] * mine_ref.shape[3]
    for g in range(rows_ref.shape[0]):
        rows = rows_ref[g]
        rows_im = jnp.concatenate([rows[:, DIRS:], -rows[:, :DIRS]], axis=1)
        for z in range(zlo_count):
            own = mine_ref[:, z, g].reshape(-1, mine_ref.shape[-1])
            other = theirs_ref[:, z, g].reshape(-1, mine_ref.shape[-1])
            cols = jnp.where(
                first,
                jnp.concatenate([own, other], axis=0),
                jnp.concatenate([other, own], axis=0),
            )
            out_ref[0, g, :, z * block : (z + 1) * block] = dot(rows, cols)
            out_ref[1, g, :, z * block : (z + 1) * block] = dot(rows_im, cols)


def cross_spectra(rows, mine, theirs):
    freqs, row_count, width = rows.shape
    col_count = 2 * mine.shape[0] * mine.shape[1] * mine.shape[3]
    core = lax.axis_index("core").astype(jnp.int32).reshape(1)
    col_spec = pl.BlockSpec(mine.shape[:2] + (FREQ_BLOCK,) + mine.shape[3:], lambda f: (0, 0, f, 0, 0))
    return pl.pallas_call(
        spec_kernel,
        out_shape=jax.ShapeDtypeStruct((2, freqs, row_count, col_count), jnp.float32),
        grid=(freqs // FREQ_BLOCK,),
        in_specs=[
            pl.BlockSpec(memory_space=pltpu.SMEM),
            pl.BlockSpec((FREQ_BLOCK, row_count, width), lambda f: (f, 0, 0)),
            col_spec,
            col_spec,
        ],
        out_specs=pl.BlockSpec((2, FREQ_BLOCK, row_count, col_count), lambda f: (0, f, 0, 0)),
        compiler_params=pltpu.CompilerParams(dimension_semantics=("arbitrary",)),
    )(core, rows, mine, theirs)


def gather_by_permutes(piece, axis_name, count):
    ahead = [piece]
    for shift in range(1, count):
        ahead.append(
            lax.ppermute(piece, axis_name, perm=[(i, (i - shift) % count) for i in range(count)])
        )
    return jnp.roll(jnp.stack(ahead), lax.axis_index(axis_name), axis=0)


def gather_by_all_to_all(piece, axis_name, count):
    copies = jnp.broadcast_to(piece[None], (count,) + piece.shape)
    return lax.all_to_all(copies, axis_name, split_axis=0, concat_axis=0)


def from_other_half(piece):
    ys = lax.axis_size("y")
    flat = [(z, y) for z in range(lax.axis_size("zhi")) for y in range(ys)]
    ahead = []
    for shift in range(ys):
        perm = [(z * ys + y, (1 - z) * ys + (y - shift) % ys) for z, y in flat]
        ahead.append(lax.ppermute(piece, ("zhi", "y"), perm=perm))
    return jnp.roll(jnp.stack(ahead), lax.axis_index("y"), axis=0)


def join_rows(same_half, other_half):
    first = lax.axis_index("zhi") == 0
    halves = jnp.where(first, jnp.stack([same_half, other_half]), jnp.stack([other_half, same_half]))
    freqs, piece, width = halves.shape[2:]
    halves = halves.reshape(-1, freqs, piece, width)
    return halves.transpose(1, 0, 2, 3).reshape(freqs, -1, width)


def local(freq_resp, node_coords, heading_steps, spectral_weights):
    project = (
        node_coords[0][:, None] * heading_steps[0][None, :]
        + node_coords[1][:, None] * heading_steps[1][None, :]
    )
    spread = jnp.sqrt(spectral_weights.astype(jnp.float32) / (64.0 * DIRS))
    partial_amp = partial_amplitudes(freq_resp, project, spread)
    amplitudes = lax.psum_scatter(partial_amp, ("zlo", "core"), scatter_dimension=1, tiled=True).astype(
        jnp.bfloat16
    )
    mine, theirs, rows = gather_cols(amplitudes)
    return cross_spectra(rows, mine, theirs)[:, :, None]


def solution(mesh):
    from jax.sharding import Mesh
    fine = Mesh(mesh.devices.reshape(4, 2, 4, 2, 4), ("zlo", "core", "drow", "zhi", "y"))
    placed = (P(None, None, ("drow", "zhi", "y"), ("zlo", "core")), P(None, ("zlo", "core")), P(), P())
    return jax.shard_map(
        local,
        mesh=fine,
        in_specs=placed,
        out_specs=P(None, None, "drow", ("zlo", "core"), ("zhi", "y")),
        check_vma=False,
    )
```

```python
import math

import jax
import jax.numpy as jnp
from jax import lax
from jax.experimental import pallas as pl
from jax.experimental.pallas import tpu as pltpu
from jax.sharding import PartitionSpec as P

DIRS = 512
FREQS = 8
GRID = 1024
NODE_TILE = 512
FREQ_BLOCK = 4


def unit_phasor(turn):
    quarter = GRID // 4
    shifted = (turn + quarter // 2) & (GRID - 1)
    quadrant = shifted >> 8
    offset = (shifted & (quarter - 1)) - quarter // 2
    x = offset.astype(jnp.float32) * (2.0 * math.pi / GRID)
    x2 = x * x
    s = x * (1.0 + x2 * (-1.0 / 6 + x2 * (1.0 / 120 + x2 * (-1.0 / 5040 + x2 * (1.0 / 362880)))))
    c = 1.0 + x2 * (-0.5 + x2 * (1.0 / 24 + x2 * (-1.0 / 720 + x2 * (1.0 / 40320))))
    odd = (quadrant & 1) == 1
    cos_mag = jnp.where(odd, s, c)
    sin_mag = jnp.where(odd, c, s)
    cos_neg = (quadrant == 1) | (quadrant == 2)
    sin_neg = quadrant >= 2
    return jnp.where(cos_neg, -cos_mag, cos_mag), jnp.where(sin_neg, -sin_mag, sin_mag)


def amp_kernel(proj_ref, spread_ref, resp_ref, out_ref):
    @pl.when(pl.program_id(0) == 0)
    def _():
        out_ref[...] = jnp.zeros_like(out_ref)

    proj = proj_ref[...]
    base_c, base_s = unit_phasor(proj & (GRID - 1))
    rows = resp_ref.shape[2]
    cos_f, sin_f = base_c, base_s
    for f in range(FREQS):
        if f > 0:
            cos_f, sin_f = (
                cos_f * base_c - sin_f * base_s,
                sin_f * base_c + cos_f * base_s,
            )
        spread = spread_ref[f : f + 1, :]
        load_re = (spread * cos_f).astype(jnp.bfloat16)
        load_im = (-spread * sin_f).astype(jnp.bfloat16)
        resp = resp_ref[:, f].reshape(2 * rows, resp_ref.shape[3])
        by_re = jnp.dot(resp, load_re, preferred_element_type=jnp.float32)
        by_im = jnp.dot(resp, load_im, preferred_element_type=jnp.float32)
        out_ref[f, :, :DIRS] += by_re[:rows] - by_im[rows:]
        out_ref[f, :, DIRS:] += by_im[:rows] + by_re[rows:]


def partial_amplitudes(freq_resp, project, spread):
    nodes = project.shape[0]
    rows = freq_resp.shape[2]
    return pl.pallas_call(
        amp_kernel,
        out_shape=jax.ShapeDtypeStruct((FREQS, rows, 2 * DIRS), jnp.float32),
        grid=(nodes // NODE_TILE,),
        in_specs=[
            pl.BlockSpec((NODE_TILE, DIRS), lambda j: (j, 0)),
            pl.BlockSpec((FREQS, DIRS), lambda j: (0, 0)),
            pl.BlockSpec((2, FREQS, rows, NODE_TILE), lambda j: (0, 0, 0, j)),
        ],
        out_specs=pl.BlockSpec((FREQS, rows, 2 * DIRS), lambda j: (0, 0, 0)),
        compiler_params=pltpu.CompilerParams(dimension_semantics=("arbitrary",)),
    )(project, spread, freq_resp)


def gather_cols(amplitudes):
    freqs, piece, width = amplitudes.shape
    along_z = gather_by_permutes(amplitudes, "zlo", lax.axis_size("zlo"))
    same_half = gather_by_permutes(amplitudes, "y", lax.axis_size("y"))
    along_z, same_half, amplitudes = lax.optimization_barrier((along_z, same_half, amplitudes))
    other_half = from_other_half(amplitudes)
    mine = lax.all_gather(along_z, "drow", axis=0)
    mine, other_half = lax.optimization_barrier((mine, other_half))
    rows = join_rows(same_half, other_half)
    theirs = lax.ppermute(mine, "core", perm=[(0, 1), (1, 0)])
    return mine, theirs, rows


def spec_kernel(core_ref, rows_ref, mine_ref, theirs_ref, out_ref):
    first = core_ref[0] == 0
    contract = (((1,), (1,)), ((), ()))

    def dot(a, b):
        return lax.dot_general(a, b, contract, preferred_element_type=jnp.float32)

    zlo_count = mine_ref.shape[1]
    block = 2 * mine_ref.shape[0] * mine_ref.shape[3]
    for g in range(rows_ref.shape[0]):
        rows = rows_ref[g]
        rows_im = jnp.concatenate([rows[:, DIRS:], -rows[:, :DIRS]], axis=1)
        for z in range(zlo_count):
            own = mine_ref[:, z, g].reshape(-1, mine_ref.shape[-1])
            other = theirs_ref[:, z, g].reshape(-1, mine_ref.shape[-1])
            cols = jnp.where(
                first,
                jnp.concatenate([own, other], axis=0),
                jnp.concatenate([other, own], axis=0),
            )
            out_ref[0, g, :, z * block : (z + 1) * block] = dot(rows, cols)
            out_ref[1, g, :, z * block : (z + 1) * block] = dot(rows_im, cols)


def cross_spectra(rows, mine, theirs):
    freqs, row_count, width = rows.shape
    col_count = 2 * mine.shape[0] * mine.shape[1] * mine.shape[3]
    core = lax.axis_index("core").astype(jnp.int32).reshape(1)
    col_spec = pl.BlockSpec(mine.shape[:2] + (FREQ_BLOCK,) + mine.shape[3:], lambda f: (0, 0, f, 0, 0))
    return pl.pallas_call(
        spec_kernel,
        out_shape=jax.ShapeDtypeStruct((2, freqs, row_count, col_count), jnp.float32),
        grid=(freqs // FREQ_BLOCK,),
        in_specs=[
            pl.BlockSpec(memory_space=pltpu.SMEM),
            pl.BlockSpec((FREQ_BLOCK, row_count, width), lambda f: (f, 0, 0)),
            col_spec,
            col_spec,
        ],
        out_specs=pl.BlockSpec((2, FREQ_BLOCK, row_count, col_count), lambda f: (0, f, 0, 0)),
        compiler_params=pltpu.CompilerParams(dimension_semantics=("arbitrary",)),
    )(core, rows, mine, theirs)


def gather_by_permutes(piece, axis_name, count):
    ahead = [piece]
    for shift in range(1, count):
        ahead.append(
            lax.ppermute(piece, axis_name, perm=[(i, (i - shift) % count) for i in range(count)])
        )
    return jnp.roll(jnp.stack(ahead), lax.axis_index(axis_name), axis=0)


def gather_by_all_to_all(piece, axis_name, count):
    copies = jnp.broadcast_to(piece[None], (count,) + piece.shape)
    return lax.all_to_all(copies, axis_name, split_axis=0, concat_axis=0)


def from_other_half(piece):
    ys = lax.axis_size("y")
    flat = [(z, y) for z in range(lax.axis_size("zhi")) for y in range(ys)]
    ahead = []
    for shift in range(ys):
        perm = [(z * ys + y, (1 - z) * ys + (y - shift) % ys) for z, y in flat]
        ahead.append(lax.ppermute(piece, ("zhi", "y"), perm=perm))
    return jnp.roll(jnp.stack(ahead), lax.axis_index("y"), axis=0)


def join_rows(same_half, other_half):
    first = lax.axis_index("zhi") == 0
    halves = jnp.where(first, jnp.stack([same_half, other_half]), jnp.stack([other_half, same_half]))
    freqs, piece, width = halves.shape[2:]
    halves = halves.reshape(-1, freqs, piece, width)
    return halves.transpose(1, 0, 2, 3).reshape(freqs, -1, width)


def local(freq_resp, node_coords, heading_steps, spectral_weights):
    project = (
        node_coords[0][:, None] * heading_steps[0][None, :]
        + node_coords[1][:, None] * heading_steps[1][None, :]
    )
    spread = jnp.sqrt(spectral_weights.astype(jnp.float32) / (64.0 * DIRS))
    partial_amp = partial_amplitudes(freq_resp, project, spread)
    amplitudes = lax.psum_scatter(partial_amp, ("zlo", "core"), scatter_dimension=1, tiled=True).astype(
        jnp.bfloat16
    )
    mine, theirs, rows = gather_cols(amplitudes)
    return cross_spectra(rows, mine, theirs)[:, :, None]


def solution(mesh):
    from jax.sharding import Mesh
    fine = Mesh(mesh.devices.reshape(4, 2, 4, 2, 4), ("zlo", "core", "drow", "zhi", "y"))
    placed = (P(None, None, ("drow", "zhi", "y"), ("zlo", "core")), P(None, ("zlo", "core")), P(), P())
    return jax.shard_map(
        local,
        mesh=fine,
        in_specs=placed,
        out_specs=P(None, None, "drow", ("zlo", "core"), ("zhi", "y")),
        check_vma=False,
    )
```
